256 devices in a mesh: expert: 16 (over y_hi, z), mp: 8 (over y_lo, x), batch: 2 (over core).
Axes of the slice: x: 4, y: 4 (y_hi: 2, y_lo: 2; y = y_hi * 2 + y_lo), z: 8, core: 2. Of those that a mesh axis runs over, the one named last changes fastest.
Arguments:
- tokens: bfloat16 [2, 2048, 2880], P('batch', 'expert', 'mp'), may hold values from -6 to 6
- segments: int32 [2, 2048], P('batch'), may hold values from 0 to 63, never falling along the last dimension, each value on 1 to 1024 neighbouring positions
- attn_gain: float32 [2880], replicated, may hold values from 0.6 to 9
- w_query: bfloat16 [2880, 4096], P('expert', 'mp'), may hold values from -0.109375 to 0.109375
- key_weight: bfloat16 [2880, 512], P('expert', 'mp'), may hold values from -0.109375 to 0.109375
- value_weight: bfloat16 [2880, 512], P('expert', 'mp'), may hold values from -0.109375 to 0.109375
- w_out: bfloat16 [4096, 2880], P('mp', 'expert'), may hold values from -0.09375 to 0.09375
- sink_head_logit: float32 [64], P('mp'), may hold values from -4 to 4
- moe_gain: float32 [2880], replicated, may hold values from 0.5 to 1.5
- expert_in: bfloat16 [16, 2, 2880, 2880], P('expert', None, None, 'mp'), may hold values from -0.3125 to 0.3125
- expert_down: bfloat16 [16, 2880, 2880], P('expert', 'mp'), may hold values from -0.01953125 to 0.01953125
- routes: int32 [2, 2048, 4], P('batch', 'expert'), may hold values from 0 to 15, all different within a row; in each aligned block of 128 rows (0 to 127, 128 to 255, ..., all dimensions but the last counted through in order) at most 48 rows name the same one
- route_weights: float32 [2, 2048, 4], P('batch', 'expert'), may hold values from 0.1 to 1
Outputs:
- hidden: bfloat16 [2, 2048, 2880], P('batch', 'expert', 'mp')
- key_cache: bfloat16 [2, 2048, 512], P('batch', 'expert', 'mp')
- value_cache: bfloat16 [2, 2048, 512], P('batch', 'expert', 'mp')
The draws below stay inside these ranges and needn't reach their ends.
Inputs may be any that keep to these rules, and one draw needn't show every extreme that they name: Within each aligned block of 128 tokens of a micro-batch (the tokens of one index of expert), no expert is named by more than 48 routes; a token's routes name different experts. `segments`: segment numbers never fall along a micro-batch; one segment holds at most 1024 tokens.
All inputs are finite; a program needn't handle non-finite values.
Results may differ from the reference program's by a relative error of at most 0.024.
The reference program's roundings to bfloat16 on the way count: a program that leaves them out, or rounds other values in their place, can miss the bound.
Values may be sent and summed in bfloat16 or wider, within the bound.
No kernel may reach another device: no remote copies, remote signals or barrier semaphores. Data moves between devices by JAX's collectives and lax.ppermute only.
A program may use at most 64 MiB of HBM per device.

```python
import math
import jax
import jax.numpy as jnp
import numpy as np
from jax import lax

MODEL_DIMENSION = 2880
QUERY_HEADS = 64
KEY_VALUE_HEADS = 8
HEAD_SIZE = 64
FF = 2880
TOP = 4
TOK_DEV = 128
EXPERTS = 16
MICRO_TOKENS = 2048
MICRO = 2
CAP = 48
N_EXPERT = 16
N_MP = 8


def draw_attn_gain(key, part):
    return jax.random.uniform(key, (MODEL_DIMENSION,), jnp.float32, 0.6, 1.6)


def block_levels(rng, shape, shards, smallest, largest):
    level, own = 1.0, jax.random.fold_in(rng, 6)
    for dim, blocks in shards:
        heights = jnp.exp(jax.random.uniform(jax.random.fold_in(own, dim), (blocks,), jnp.float32, smallest / len(shards), largest / len(shards)))
        level = level * jnp.repeat(heights, shape[dim] // blocks).reshape([-1 if axis == dim else 1 for axis in range(len(shape))])
    return level


def length_profile(count, total, limit, slope):
    loads = [(1 << 20) // math.isqrt(standing ** slope) + 1 for standing in range(2, count + 1)]
    spare, holding = total - limit - (count - 1), [1] * (count - 1)
    while spare > 0:
        free = [i for i in range(count - 1) if holding[i] < limit]
        whole, remaining = sum([loads[i] for i in free]), spare
        for i in free:
            more = min(limit - holding[i], max(1, remaining * loads[i] // whole), spare)
            holding[i] = holding[i] + more
            spare = spare - more
    return np.array([limit] + holding)


def uneven_parts(stream_key, count, total, reach, skew):
    if count == 2:
        one = jax.random.randint(stream_key, (), max(1, total - reach), min(reach, total - 1) + 1)
        return jnp.stack([one, total - one])
    sizes = jnp.asarray(length_profile(count, total, reach, skew), jnp.int32)
    couples = (count - 1) // 2
    donor, taker = sizes[1:1 + 2 * couples:2], sizes[2:2 + 2 * couples:2]
    slack = jnp.minimum(donor - 1, reach - taker)
    moved = jax.random.randint(jax.random.fold_in(stream_key, 1), (couples,), 0, 1 << 20) % (slack + 1)
    sizes = sizes.at[1:1 + 2 * couples:2].set(donor - moved).at[2:2 + 2 * couples:2].set(taker + moved)
    return sizes[jax.random.permutation(jax.random.fold_in(stream_key, 2), count)]


def shared_out(rng, own, number, rows, number_of, top, reach, slope):
    order = jax.random.permutation(rng, number_of)
    crowded, usual = load_shares(number_of, rows * top, reach, slope, True), load_shares(number_of, rows * top, reach, slope, False)
    places = jnp.arange(number_of)

    def named(lengths, turn):
        used = int((lengths > 0).sum())
        fixed = max(1, used // 4)
        moved = fixed + (places - fixed + turn * (used - fixed)) % max(1, number_of - fixed)
        return jnp.zeros((number_of,), jnp.int32).at[order[jnp.where(places < fixed, places, moved)]].set(jnp.asarray(lengths, jnp.int32))

    lengths = jnp.where(number % 4 == 0, named(crowded, number // 4), named(usual, number - number // 4 - 1))
    mixed = jax.random.permutation(jax.random.fold_in(own, 3), number_of)
    donor, taker = mixed[0:number_of // 2 * 2:2], mixed[1:number_of // 2 * 2:2]
    slack = jnp.minimum(lengths[donor] - 1, reach - lengths[taker]) // 2
    slack = jnp.where((donor == order[0]) | (taker == order[0]) | (lengths[taker] == 0), 0, jnp.maximum(slack, 0))
    moved = jax.random.randint(jax.random.fold_in(own, 4), (number_of // 2,), 0, 1 << 20) % (slack + 1)
    lengths = lengths.at[donor].add(-moved).at[taker].add(moved)
    members = jnp.searchsorted(jnp.cumsum(lengths), jnp.arange(rows * top), side="right").astype(jnp.int32)
    grid = members.reshape(top, rows).T
    grid = grid[jax.random.permutation(jax.random.fold_in(own, 1), rows)]
    turn = jax.random.randint(jax.random.fold_in(own, 2), (rows, 1), 0, top)
    return jnp.take_along_axis(grid, (jnp.arange(top)[None, :] + turn) % top, axis=1)


def load_shares(number_of, total, reach, skew, full):
    weights = [(1 << 20) // math.isqrt(grade ** skew) + 1 for grade in range(1, number_of + 1)]
    largest = reach if full else min(reach, max(-(-total // number_of), total * weights[0] // sum(weights)))
    least = 1 if total - largest >= number_of - 1 else 0
    counts, rest = [largest] + [least] * (number_of - 1), total - largest - least * (number_of - 1)
    while rest > 0:
        movable = [i for i in range(1, number_of) if counts[i] < largest] or [i for i in range(1, number_of) if counts[i] < reach]
        mass, budget = sum([weights[i] for i in movable]), rest
        for i in movable:
            extra = min(reach - counts[i], max(1, budget * weights[i] // mass), rest)
            counts[i] = counts[i] + extra
            rest = rest - extra
    return np.array(counts)


def scatter_about(rng, dims, deviation, limit, cuts=(), kind=jnp.bfloat16):
    level = block_levels(rng, dims, cuts, -0.22, 0.18) if cuts else 1.0
    entries = jax.random.normal(rng, dims, jnp.float32) * deviation * level
    return jnp.minimum(jnp.maximum(entries, -limit), limit).astype(kind)


def setup_inputs(seed: int = 0) -> dict:
    arg_keys = jax.random.split(jax.random.key(seed), 14)
    tokens = scatter_about(arg_keys[0], (MICRO, MICRO_TOKENS, MODEL_DIMENSION), 1.0, 6.0, ((0, 2), (1, 16), (2, 8)))
    segments = jax.vmap(lambda own: jnp.searchsorted(jnp.cumsum(uneven_parts(own, MICRO_TOKENS // 32, MICRO_TOKENS, MICRO_TOKENS // 2, 2)), jnp.arange(MICRO_TOKENS), side="right"))(jax.random.split(arg_keys[1], MICRO)).reshape((MICRO, MICRO_TOKENS)).astype(jnp.int32)
    attn_gain = draw_attn_gain(jax.random.fold_in(arg_keys[13], 71), 0)
    w_query = scatter_about(arg_keys[3], (MODEL_DIMENSION, QUERY_HEADS * HEAD_SIZE), MODEL_DIMENSION ** -0.5, 0.109375, ((0, 16), (1, 8)))
    key_weight = scatter_about(arg_keys[4], (MODEL_DIMENSION, KEY_VALUE_HEADS * HEAD_SIZE), MODEL_DIMENSION ** -0.5, 0.109375, ((0, 16), (1, 8)))
    value_weight = scatter_about(arg_keys[5], (MODEL_DIMENSION, KEY_VALUE_HEADS * HEAD_SIZE), MODEL_DIMENSION ** -0.5, 0.109375, ((0, 16), (1, 8)))
    w_out = scatter_about(arg_keys[6], (QUERY_HEADS * HEAD_SIZE, MODEL_DIMENSION), (QUERY_HEADS * HEAD_SIZE) ** -0.5, 0.09375, ((0, 8), (1, 16)))
    sink_head_logit = scatter_about(arg_keys[7], (QUERY_HEADS,), 1.0, 4.0, ((0, 8),), jnp.float32)
    moe_gain = jnp.clip(1.0 + 0.1 * jax.random.normal(arg_keys[8], (MODEL_DIMENSION,), jnp.float32), 0.5, 1.5)
    expert_in = scatter_about(arg_keys[9], (EXPERTS, 2, MODEL_DIMENSION, FF), (MODEL_DIMENSION // 9) ** -0.5, 0.3125, ((0, 16), (3, 8)))
    expert_down = scatter_about(arg_keys[10], (EXPERTS, FF, MODEL_DIMENSION), (FF * 36) ** -0.5, 0.01953125, ((0, 16), (1, 8)))
    routes_keys = jax.random.split(jax.random.fold_in(arg_keys[11], 1), MICRO * MICRO_TOKENS // TOK_DEV)
    routes_turns = jax.random.permutation(jax.random.fold_in(arg_keys[11], 3), MICRO * MICRO_TOKENS // TOK_DEV)
    routes = jax.vmap(lambda own, number: shared_out(jax.random.fold_in(arg_keys[11], 2), own, number, TOK_DEV, EXPERTS, TOP, CAP, 2))(routes_keys, routes_turns).reshape((MICRO, MICRO_TOKENS, TOP))
    route_weights = jnp.clip(0.1 + 0.9 * jax.random.uniform(arg_keys[12], (MICRO, MICRO_TOKENS, TOP), jnp.float32) ** block_levels(arg_keys[12], (MICRO, MICRO_TOKENS, TOP), ((0, 2), (1, 16)), -0.2, 0.2), 0.1, 1.0)
    return {"tokens": tokens, "segments": segments, "attn_gain": attn_gain, "w_query": w_query, "key_weight": key_weight, "value_weight": value_weight, "w_out": w_out, "sink_head_logit": sink_head_logit, "moe_gain": moe_gain, "expert_in": expert_in, "expert_down": expert_down, "routes": routes, "route_weights": route_weights}


eps = 1e-05
rope_base = 150000.0
clamp_limit = 7.0
glu_alpha = 1.702

def rms_norm(row_block, gain):
    values = row_block.astype(jnp.float32)
    inv_scale = lax.rsqrt(lax.optimization_barrier(jnp.mean(values * values, axis=-1, keepdims=True)) + eps)
    return (values * inv_scale * gain.astype(jnp.float32)).astype(jnp.bfloat16)

def apply_rotary(values, token_positions):
    half_dim = values.shape[-1] // 2
    inv_freq = jnp.power(rope_base, -2.0 * jnp.arange(half_dim, dtype=jnp.float32) / values.shape[-1])
    rot_angle = token_positions.astype(jnp.float32)[:, None] * inv_freq[None, :]
    cosine = jnp.cos(rot_angle)[:, None, :]
    sine_val = jnp.sin(rot_angle)[:, None, :]
    first_half = values[..., :half_dim]
    second_half = values[..., half_dim:]
    return jnp.concatenate([first_half * cosine - second_half * sine_val, second_half * cosine + first_half * sine_val], axis=-1)

def attend(query_matrix, key_rotary, value_fresh, seg_ids, sink_head_logit):
    heads_per_group = QUERY_HEADS // KEY_VALUE_HEADS
    block_len = math.gcd(MICRO_TOKENS, 256)
    key_by_head = key_rotary.reshape(MICRO_TOKENS, KEY_VALUE_HEADS, HEAD_SIZE).astype(jnp.float32).transpose(1, 0, 2)
    value_by_head = value_fresh.reshape(MICRO_TOKENS, KEY_VALUE_HEADS, HEAD_SIZE).astype(jnp.float32).transpose(1, 0, 2)
    query_by_head = query_matrix.astype(jnp.float32).reshape(MICRO_TOKENS, KEY_VALUE_HEADS, heads_per_group, HEAD_SIZE).transpose(1, 2, 0, 3)
    sink_scores = sink_head_logit.astype(jnp.float32).reshape(KEY_VALUE_HEADS, heads_per_group)[:, :, None]
    key_pos = jnp.arange(MICRO_TOKENS, dtype=jnp.int32)

    def one_block(index):
        first_row = index * block_len
        query_part = lax.dynamic_slice_in_dim(query_by_head, first_row, block_len, 2)
        query_pos = first_row + jnp.arange(block_len, dtype=jnp.int32)
        query_seg = lax.dynamic_slice_in_dim(seg_ids, first_row, block_len, 0)
        scores = jnp.einsum('hgqd,hkd->hgqk', query_part, key_by_head) * HEAD_SIZE ** (-0.5)
        allowed = (key_pos[None, :] <= query_pos[:, None]) & (seg_ids[None, :] == query_seg[:, None])
        scores = jnp.where(allowed[None, None], scores, -jnp.inf)
        top_val = jnp.maximum(lax.optimization_barrier(jnp.max(scores, axis=-1)), sink_scores)
        probs = jnp.exp(scores - top_val[..., None]).astype(jnp.bfloat16)
        denom = lax.optimization_barrier(jnp.sum(probs.astype(jnp.float32), axis=-1)) + jnp.exp(sink_scores - top_val)
        mixed = jnp.einsum('hgqk,hkd->hgqd', probs.astype(jnp.float32), value_by_head) / denom[..., None]
        return mixed.astype(jnp.bfloat16).transpose(2, 0, 1, 3).reshape(block_len, QUERY_HEADS * HEAD_SIZE)
    outputs = lax.map(one_block, jnp.arange(MICRO_TOKENS // block_len, dtype=jnp.int32))
    return outputs.reshape(MICRO_TOKENS, QUERY_HEADS * HEAD_SIZE)

def expert_rows(row_block, w_in, w_down):
    gate_val = jnp.dot(row_block, w_in[0], preferred_element_type=jnp.float32)
    up_val = jnp.dot(row_block, w_in[1], preferred_element_type=jnp.float32)
    gate_val = jnp.minimum(gate_val, clamp_limit)
    up_val = jnp.clip(up_val, -clamp_limit, clamp_limit)
    activated = ((up_val + 1.0) * gate_val * jax.nn.sigmoid(glu_alpha * gate_val)).astype(jnp.bfloat16)
    row_count = row_block.shape[0]
    pieces = activated.reshape(row_count, N_MP, FF // N_MP).astype(jnp.float32)
    downs = w_down.reshape(N_MP, FF // N_MP, MODEL_DIMENSION).astype(jnp.float32)
    partial_value = jnp.einsum('pnf,nfd->pnd', pieces, downs).astype(jnp.bfloat16)
    partial_value = lax.optimization_barrier(partial_value)
    return lax.optimization_barrier(jnp.sum(partial_value.astype(jnp.float32), axis=1)).astype(jnp.bfloat16)

def reference(tokens, segments, attn_gain, w_query, key_weight, value_weight, w_out, sink_head_logit, moe_gain, expert_in, expert_down, routes, route_weights):
    token_positions = jnp.arange(MICRO_TOKENS, dtype=jnp.int32)
    first_list = []
    key_list = []
    value_list = []
    for micro_index in range(MICRO):
        x_micro = tokens[micro_index]
        input_normalised = rms_norm(x_micro, attn_gain)
        query_matrix = apply_rotary(jnp.dot(input_normalised, w_query, preferred_element_type=jnp.float32).reshape(MICRO_TOKENS, QUERY_HEADS, HEAD_SIZE), token_positions).astype(jnp.bfloat16)
        key_rotary = apply_rotary(jnp.dot(input_normalised, key_weight, preferred_element_type=jnp.float32).reshape(MICRO_TOKENS, KEY_VALUE_HEADS, HEAD_SIZE), token_positions).astype(jnp.bfloat16).reshape(MICRO_TOKENS, KEY_VALUE_HEADS * HEAD_SIZE)
        value_fresh = jnp.dot(input_normalised, value_weight, preferred_element_type=jnp.float32).astype(jnp.bfloat16)
        mixed = attend(query_matrix, key_rotary, value_fresh, segments[micro_index], sink_head_logit)
        first_out = (x_micro.astype(jnp.float32) + jnp.dot(mixed, w_out, preferred_element_type=jnp.float32)).astype(jnp.bfloat16)
        first_list.append(first_out)
        key_list.append(key_rotary)
        value_list.append(value_fresh)
    first_all = jnp.stack(first_list, axis=0)
    block_total = MICRO * N_EXPERT
    assigned = TOK_DEV * TOP
    moe_in = rms_norm(first_all, moe_gain).reshape(block_total * TOK_DEV, MODEL_DIMENSION)
    chosen = routes.reshape(block_total, assigned)
    onehot = (chosen[..., None] == jnp.arange(EXPERTS, dtype=jnp.int32)[None, None, :]).astype(jnp.int32)
    ranks = lax.optimization_barrier(jnp.sum((jnp.cumsum(onehot, axis=1) - onehot) * onehot, axis=2))
    place = jnp.arange(block_total, dtype=jnp.int32)[:, None] * CAP + ranks
    token_row = jnp.arange(block_total, dtype=jnp.int32)[:, None] * TOK_DEV + (jnp.arange(assigned, dtype=jnp.int32) // TOP)[None, :]
    table = jnp.full((EXPERTS, block_total * CAP), block_total * TOK_DEV, jnp.int32).at[chosen, place].set(token_row)
    padded = jnp.concatenate([moe_in, jnp.zeros((1, MODEL_DIMENSION), jnp.bfloat16)], axis=0)

    def run_expert(index):
        return expert_rows(padded[table[index]], expert_in[index], expert_down[index])
    outputs = lax.map(run_expert, jnp.arange(EXPERTS, dtype=jnp.int32))
    picked = outputs[chosen, place].astype(jnp.float32).reshape(block_total, TOK_DEV, TOP, MODEL_DIMENSION)
    moe_sum = lax.optimization_barrier(jnp.sum(picked * route_weights.reshape(block_total, TOK_DEV, TOP, 1), axis=2))
    hidden = (first_all.reshape(block_total, TOK_DEV, MODEL_DIMENSION).astype(jnp.float32) + moe_sum).astype(jnp.bfloat16).reshape(MICRO, MICRO_TOKENS, MODEL_DIMENSION)
    return (hidden, jnp.stack(key_list, axis=0), jnp.stack(value_list, axis=0))
```

```python
import math

import jax
import jax.numpy as jnp
from jax import lax
from jax.sharding import PartitionSpec as P

HEAD_SIZE = 64


eps = 1e-05
rope_base = 150000.0
clamp_limit = 7.0
glu_alpha = 1.702


def rms_norm(row_block, gain):
    values = row_block.astype(jnp.float32)
    inv_scale = lax.rsqrt(jnp.mean(values * values, axis=-1, keepdims=True) + eps)
    return (values * inv_scale * gain).astype(jnp.bfloat16)


def apply_rotary(values, token_positions):
    half_dim = values.shape[-1] // 2
    inv_freq = jnp.power(
        rope_base, -2.0 * jnp.arange(half_dim, dtype=jnp.float32) / values.shape[-1]
    )
    rot_angle = token_positions.astype(jnp.float32)[:, None] * inv_freq[None, :]
    cosine = jnp.cos(rot_angle)[:, None, :]
    sine_val = jnp.sin(rot_angle)[:, None, :]
    first_half = values[..., :half_dim]
    second_half = values[..., half_dim:]
    return jnp.concatenate(
        [
            first_half * cosine - second_half * sine_val,
            second_half * cosine + first_half * sine_val,
        ],
        axis=-1,
    )


def expert_rows(row_block, w_in, w_down):
    gate_val = jnp.dot(row_block, w_in[0], preferred_element_type=jnp.float32)
    up_val = jnp.dot(row_block, w_in[1], preferred_element_type=jnp.float32)
    gate_val = jnp.minimum(gate_val, clamp_limit)
    up_val = jnp.clip(up_val, -clamp_limit, clamp_limit)
    activated = ((up_val + 1.0) * gate_val * jax.nn.sigmoid(glu_alpha * gate_val)).astype(
        jnp.bfloat16
    )
    return jnp.dot(activated, w_down, preferred_element_type=jnp.float32)


def shards(
    tokens,
    segments,
    attn_gain,
    w_query,
    key_weight,
    value_weight,
    w_out,
    sink_head_logit,
    moe_gain,
    expert_in,
    expert_down,
    routes,
    route_weights,
):
    local_rows = tokens[0]
    tok_count = local_rows.shape[0]
    expert_devs = lax.axis_size("expert")
    row_start = lax.axis_index("expert") * tok_count
    whole_rows = lax.all_gather(local_rows, "mp", axis=1, tiled=True)
    input_normalised = rms_norm(whole_rows, attn_gain)
    query_cols = w_query.shape[1]
    kv_cols = key_weight.shape[1]
    query_weight = lax.all_gather(w_query, "expert", axis=0, tiled=True)
    kv_weight = lax.all_gather(
        jnp.concatenate([key_weight, value_weight], axis=1), "expert", axis=0, tiled=True
    )
    query_raw = jnp.dot(input_normalised, query_weight, preferred_element_type=jnp.float32)
    kv_raw = jnp.dot(input_normalised, kv_weight, preferred_element_type=jnp.float32)
    key_raw = kv_raw[:, :kv_cols]
    value_raw = kv_raw[:, kv_cols:]
    token_positions = row_start + jnp.arange(tok_count, dtype=jnp.int32)
    query_by_head = query_cols // HEAD_SIZE
    kv_heads = kv_cols // HEAD_SIZE
    heads_per_group = query_by_head // kv_heads
    query_matrix = apply_rotary(
        query_raw.reshape(tok_count, query_by_head, HEAD_SIZE), token_positions
    ).astype(jnp.bfloat16)
    key_rotary = (
        apply_rotary(key_raw.reshape(tok_count, kv_heads, HEAD_SIZE), token_positions)
        .astype(jnp.bfloat16)
        .reshape(tok_count, kv_cols)
    )
    value_fresh = value_raw.astype(jnp.bfloat16)
    kv_all = lax.all_gather(
        jnp.concatenate([key_rotary, value_fresh], axis=1), "expert", axis=0, tiled=True
    )
    keys_all = kv_all[:, :kv_cols]
    values_all = kv_all[:, kv_cols:]
    seq_len = keys_all.shape[0]
    seg_all = segments[0]
    seg_local = lax.dynamic_slice_in_dim(seg_all, row_start, tok_count)
    row_total = heads_per_group * tok_count
    query_rows = (
        query_matrix.reshape(tok_count, kv_heads, heads_per_group, HEAD_SIZE)
        .transpose(1, 2, 0, 3)
        .reshape(kv_heads, row_total, HEAD_SIZE)
    )
    key_by_head = keys_all.reshape(seq_len, kv_heads, HEAD_SIZE).transpose(1, 0, 2)
    value_by_head = values_all.reshape(seq_len, kv_heads, HEAD_SIZE).transpose(1, 0, 2)
    row_pos = jnp.tile(token_positions, heads_per_group)
    row_seg = jnp.tile(seg_local, heads_per_group)
    sink_rows = jnp.repeat(sink_head_logit.reshape(kv_heads, heads_per_group), tok_count, axis=1)
    key_block = math.gcd(seq_len, 512)
    block_count = seq_len // key_block
    score_scale = HEAD_SIZE ** (-0.5)

    def block_scores(index):
        key_first = index * key_block
        key_part = lax.dynamic_slice_in_dim(key_by_head, key_first, key_block, 1)
        scores = (
            jnp.einsum("hrd,hkd->hrk", query_rows, key_part, preferred_element_type=jnp.float32)
            * score_scale
        )
        key_pos = key_first + jnp.arange(key_block, dtype=jnp.int32)
        key_seg = lax.dynamic_slice_in_dim(seg_all, key_first, key_block, 0)
        allowed = (key_pos[None, :] <= row_pos[:, None]) & (key_seg[None, :] == row_seg[:, None])
        return jnp.where(allowed[None], scores, -jnp.inf)

    def max_step(index, running):
        return jnp.maximum(running, jnp.max(block_scores(index), axis=-1))

    row_max = lax.fori_loop(0, block_count, max_step, sink_rows)

    def sum_step(index, carried):
        weighted, denom = carried
        probs = jnp.exp(block_scores(index) - row_max[..., None]).astype(jnp.bfloat16)
        value_part = lax.dynamic_slice_in_dim(value_by_head, index * key_block, key_block, 1)
        weighted = weighted + jnp.einsum(
            "hrk,hkd->hrd", probs, value_part, preferred_element_type=jnp.float32
        )
        denom = denom + jnp.sum(probs, axis=-1, dtype=jnp.float32)
        return (weighted, denom)

    init_pair = (
        jnp.zeros((kv_heads, row_total, HEAD_SIZE), jnp.float32),
        jnp.zeros((kv_heads, row_total), jnp.float32),
    )
    weighted, denom = lax.fori_loop(0, block_count, sum_step, init_pair)
    denom = denom + jnp.exp(sink_rows - row_max)
    mixed = (weighted / denom[..., None]).astype(jnp.bfloat16)
    mixed = (
        mixed.reshape(kv_heads, heads_per_group, tok_count, HEAD_SIZE)
        .transpose(2, 0, 1, 3)
        .reshape(tok_count, query_cols)
    )
    out_terms = jnp.dot(
        mixed,
        lax.all_gather(w_out, "expert", axis=1, tiled=True),
        preferred_element_type=jnp.float32,
    )
    attn_part = lax.psum_scatter(
        out_terms.astype(jnp.bfloat16), "mp", scatter_dimension=1, tiled=True
    ).astype(jnp.float32)
    first_out = (local_rows.astype(jnp.float32) + attn_part).astype(jnp.bfloat16)
    top_count = routes.shape[2]
    local_experts = expert_in.shape[0]
    expert_count = local_experts * expert_devs
    capacity = 3 * tok_count * top_count // (2 * expert_count)
    chosen = routes[0].reshape(tok_count * top_count)
    onehot = (chosen[:, None] == jnp.arange(expert_count, dtype=jnp.int32)[None, :]).astype(
        jnp.int32
    )
    ranks = jnp.sum((jnp.cumsum(onehot, axis=0) - onehot) * onehot, axis=1)
    target = chosen * capacity + ranks
    source_row = (
        jnp.full((expert_count * capacity,), tok_count, jnp.int32)
        .at[target]
        .set(jnp.arange(tok_count * top_count, dtype=jnp.int32) // top_count)
    )
    padded = jnp.concatenate(
        [first_out, jnp.zeros((1, first_out.shape[1]), jnp.bfloat16)], axis=0
    )
    outgoing = padded[source_row].reshape(expert_count, capacity, padded.shape[1])
    arrived = lax.all_to_all(outgoing, "expert", split_axis=0, concat_axis=0, tiled=True)
    arrived_rows = arrived.reshape(expert_count * capacity, arrived.shape[2])
    inputs = rms_norm(lax.all_gather(arrived_rows, "mp", axis=1, tiled=True), moe_gain)
    w_in = expert_in[0]
    gate_val = jnp.dot(inputs, w_in[0], preferred_element_type=jnp.float32)
    up_val = jnp.dot(inputs, w_in[1], preferred_element_type=jnp.float32)
    gate_val = jnp.minimum(gate_val, clamp_limit)
    up_val = jnp.clip(up_val, -clamp_limit, clamp_limit)
    activated = ((up_val + 1.0) * gate_val * jax.nn.sigmoid(glu_alpha * gate_val)).astype(
        jnp.bfloat16
    )
    partials_t = lax.dot_general(
        expert_down[0], activated, (((0,), (1,)), ((), ())), preferred_element_type=jnp.float32
    )
    expert_out_t = lax.psum_scatter(
        partials_t.astype(jnp.bfloat16), "mp", scatter_dimension=0, tiled=True
    )
    local_width = expert_out_t.shape[0]
    expert_out = expert_out_t.T.reshape(expert_count, capacity, local_width)
    returned = lax.all_to_all(expert_out, "expert", split_axis=0, concat_axis=0, tiled=True)
    picked = returned.reshape(expert_count * capacity, local_width)[target].reshape(
        tok_count, top_count, local_width
    )
    moe_sum = jnp.sum(picked.astype(jnp.float32) * route_weights[0][..., None], axis=1)
    hidden = (first_out.astype(jnp.float32) + moe_sum).astype(jnp.bfloat16)
    return (hidden[None], key_rotary[None], value_fresh[None])


def solution(mesh):
    placed = (
        P("batch", "expert", "mp"),
        P("batch", None),
        P(),
        P("expert", "mp"),
        P("expert", "mp"),
        P("expert", "mp"),
        P("mp", "expert"),
        P("mp"),
        P(),
        P("expert", None, None, "mp"),
        P("expert", "mp", None),
        P("batch", "expert", None),
        P("batch", "expert", None),
    )
    return jax.shard_map(
        shards,
        mesh=mesh,
        in_specs=placed,
        out_specs=(
            P("batch", "expert", "mp"),
            P("batch", "expert", "mp"),
            P("batch", "expert", "mp"),
        ),
        check_vma=False,
    )
```

```python
import math

import jax
import jax.numpy as jnp
from jax import lax
from jax.sharding import PartitionSpec as P

HEAD_SIZE = 64


eps = 1e-05
rope_base = 150000.0
clamp_limit = 7.0
glu_alpha = 1.702


def rms_norm(row_block, gain):
    values = row_block.astype(jnp.float32)
    inv_scale = lax.rsqrt(jnp.mean(values * values, axis=-1, keepdims=True) + eps)
    return (values * inv_scale * gain).astype(jnp.bfloat16)


def apply_rotary(values, token_positions):
    half_dim = values.shape[-1] // 2
    inv_freq = jnp.power(
        rope_base, -2.0 * jnp.arange(half_dim, dtype=jnp.float32) / values.shape[-1]
    )
    rot_angle = token_positions.astype(jnp.float32)[:, None] * inv_freq[None, :]
    cosine = jnp.cos(rot_angle)[:, None, :]
    sine_val = jnp.sin(rot_angle)[:, None, :]
    first_half = values[..., :half_dim]
    second_half = values[..., half_dim:]
    return jnp.concatenate(
        [
            first_half * cosine - second_half * sine_val,
            second_half * cosine + first_half * sine_val,
        ],
        axis=-1,
    )


def swap_cores(block):
    return lax.ppermute(block, "batch", perm=[(0, 1), (1, 0)])


def expert_rows(row_block, w_in, w_down):
    gate_val = jnp.dot(row_block, w_in[0], preferred_element_type=jnp.float32)
    up_val = jnp.dot(row_block, w_in[1], preferred_element_type=jnp.float32)
    gate_val = jnp.minimum(gate_val, clamp_limit)
    up_val = jnp.clip(up_val, -clamp_limit, clamp_limit)
    activated = ((up_val + 1.0) * gate_val * jax.nn.sigmoid(glu_alpha * gate_val)).astype(
        jnp.bfloat16
    )
    return jnp.dot(activated, w_down, preferred_element_type=jnp.float32)


def shards(
    tokens,
    segments,
    attn_gain,
    w_query,
    key_weight,
    value_weight,
    w_out,
    sink_head_logit,
    moe_gain,
    expert_in,
    expert_down,
    routes,
    route_weights,
):
    local_rows = tokens[0]
    tok_count = local_rows.shape[0]
    expert_devs = lax.axis_size("expert")
    row_start = lax.axis_index("expert") * tok_count
    whole_rows = lax.all_gather(local_rows, "mp", axis=1, tiled=True)
    input_normalised = rms_norm(whole_rows, attn_gain)
    query_cols = w_query.shape[1]
    kv_cols = key_weight.shape[1]
    core = lax.axis_index("batch")
    first_core = core == 0
    half_q = query_cols // 2
    query_mine = lax.all_gather(
        lax.dynamic_slice_in_dim(w_query, core * half_q, half_q, 1), "expert", axis=0, tiled=True
    )
    query_other = swap_cores(query_mine)
    kv_mine = lax.all_gather(
        jnp.where(first_core, key_weight, value_weight), "expert", axis=0, tiled=True
    )
    kv_other = swap_cores(kv_mine)
    q_mine = jnp.dot(input_normalised, query_mine, preferred_element_type=jnp.float32)
    q_other = jnp.dot(input_normalised, query_other, preferred_element_type=jnp.float32)
    query_raw = jnp.where(
        first_core,
        jnp.concatenate([q_mine, q_other], axis=1),
        jnp.concatenate([q_other, q_mine], axis=1),
    )
    kv_mine_raw = jnp.dot(input_normalised, kv_mine, preferred_element_type=jnp.float32)
    kv_other_raw = jnp.dot(input_normalised, kv_other, preferred_element_type=jnp.float32)
    key_raw = jnp.where(first_core, kv_mine_raw, kv_other_raw)
    value_raw = jnp.where(first_core, kv_other_raw, kv_mine_raw)
    token_positions = row_start + jnp.arange(tok_count, dtype=jnp.int32)
    query_by_head = query_cols // HEAD_SIZE
    kv_heads = kv_cols // HEAD_SIZE
    heads_per_group = query_by_head // kv_heads
    query_matrix = apply_rotary(
        query_raw.reshape(tok_count, query_by_head, HEAD_SIZE), token_positions
    ).astype(jnp.bfloat16)
    key_rotary = (
        apply_rotary(key_raw.reshape(tok_count, kv_heads, HEAD_SIZE), token_positions)
        .astype(jnp.bfloat16)
        .reshape(tok_count, kv_cols)
    )
    value_fresh = value_raw.astype(jnp.bfloat16)
    kv_all = lax.all_gather(
        jnp.concatenate([key_rotary, value_fresh], axis=1), "expert", axis=0, tiled=True
    )
    keys_all = kv_all[:, :kv_cols]
    values_all = kv_all[:, kv_cols:]
    seq_len = keys_all.shape[0]
    seg_all = segments[0]
    seg_local = lax.dynamic_slice_in_dim(seg_all, row_start, tok_count)
    row_total = heads_per_group * tok_count
    query_rows = (
        query_matrix.reshape(tok_count, kv_heads, heads_per_group, HEAD_SIZE)
        .transpose(1, 2, 0, 3)
        .reshape(kv_heads, row_total, HEAD_SIZE)
    )
    key_by_head = keys_all.reshape(seq_len, kv_heads, HEAD_SIZE).transpose(1, 0, 2)
    value_by_head = values_all.reshape(seq_len, kv_heads, HEAD_SIZE).transpose(1, 0, 2)
    row_pos = jnp.tile(token_positions, heads_per_group)
    row_seg = jnp.tile(seg_local, heads_per_group)
    sink_rows = jnp.repeat(sink_head_logit.reshape(kv_heads, heads_per_group), tok_count, axis=1)
    key_block = math.gcd(seq_len, 512)
    block_count = seq_len // key_block
    score_scale = HEAD_SIZE ** (-0.5)

    def block_scores(index):
        key_first = index * key_block
        key_part = lax.dynamic_slice_in_dim(key_by_head, key_first, key_block, 1)
        scores = (
            jnp.einsum("hrd,hkd->hrk", query_rows, key_part, preferred_element_type=jnp.float32)
            * score_scale
        )
        key_pos = key_first + jnp.arange(key_block, dtype=jnp.int32)
        key_seg = lax.dynamic_slice_in_dim(seg_all, key_first, key_block, 0)
        allowed = (key_pos[None, :] <= row_pos[:, None]) & (key_seg[None, :] == row_seg[:, None])
        return jnp.where(allowed[None], scores, -jnp.inf)

    def max_step(index, running):
        return jnp.maximum(running, jnp.max(block_scores(index), axis=-1))

    row_max = lax.fori_loop(0, block_count, max_step, sink_rows)

    def sum_step(index, carried):
        weighted, denom = carried
        probs = jnp.exp(block_scores(index) - row_max[..., None]).astype(jnp.bfloat16)
        value_part = lax.dynamic_slice_in_dim(value_by_head, index * key_block, key_block, 1)
        weighted = weighted + jnp.einsum(
            "hrk,hkd->hrd", probs, value_part, preferred_element_type=jnp.float32
        )
        denom = denom + jnp.sum(probs, axis=-1, dtype=jnp.float32)
        return (weighted, denom)

    init_pair = (
        jnp.zeros((kv_heads, row_total, HEAD_SIZE), jnp.float32),
        jnp.zeros((kv_heads, row_total), jnp.float32),
    )
    weighted, denom = lax.fori_loop(0, block_count, sum_step, init_pair)
    denom = denom + jnp.exp(sink_rows - row_max)
    mixed = (weighted / denom[..., None]).astype(jnp.bfloat16)
    mixed = (
        mixed.reshape(kv_heads, heads_per_group, tok_count, HEAD_SIZE)
        .transpose(2, 0, 1, 3)
        .reshape(tok_count, query_cols)
    )
    half_o = w_out.shape[0] // 2
    out_mine = lax.all_gather(
        lax.dynamic_slice_in_dim(w_out, core * half_o, half_o, 0), "expert", axis=1, tiled=True
    )
    out_other = swap_cores(out_mine)
    mixed_mine = lax.dynamic_slice_in_dim(mixed, core * half_o, half_o, 1)
    mixed_other = lax.dynamic_slice_in_dim(mixed, (1 - core) * half_o, half_o, 1)
    out_terms = jnp.dot(mixed_mine, out_mine, preferred_element_type=jnp.float32) + jnp.dot(
        mixed_other, out_other, preferred_element_type=jnp.float32
    )
    attn_part = lax.psum_scatter(
        out_terms.astype(jnp.bfloat16), "mp", scatter_dimension=1, tiled=True
    ).astype(jnp.float32)
    first_out = (local_rows.astype(jnp.float32) + attn_part).astype(jnp.bfloat16)
    top_count = routes.shape[2]
    local_experts = expert_in.shape[0]
    expert_count = local_experts * expert_devs
    capacity = 3 * tok_count * top_count // (2 * expert_count)
    chosen = routes[0].reshape(tok_count * top_count)
    onehot = (chosen[:, None] == jnp.arange(expert_count, dtype=jnp.int32)[None, :]).astype(
        jnp.int32
    )
    ranks = jnp.sum((jnp.cumsum(onehot, axis=0) - onehot) * onehot, axis=1)
    target = chosen * capacity + ranks
    source_row = (
        jnp.full((expert_count * capacity,), tok_count, jnp.int32)
        .at[target]
        .set(jnp.arange(tok_count * top_count, dtype=jnp.int32) // top_count)
    )
    padded = jnp.concatenate(
        [first_out, jnp.zeros((1, first_out.shape[1]), jnp.bfloat16)], axis=0
    )
    outgoing = padded[source_row].reshape(expert_count, capacity, padded.shape[1])
    arrived = lax.all_to_all(outgoing, "expert", split_axis=0, concat_axis=0, tiled=True)
    arrived_rows = arrived.reshape(expert_count * capacity, arrived.shape[2])
    inputs = rms_norm(lax.all_gather(arrived_rows, "mp", axis=1, tiled=True), moe_gain)
    w_in = expert_in[0]
    gate_val = jnp.dot(inputs, w_in[0], preferred_element_type=jnp.float32)
    up_val = jnp.dot(inputs, w_in[1], preferred_element_type=jnp.float32)
    gate_val = jnp.minimum(gate_val, clamp_limit)
    up_val = jnp.clip(up_val, -clamp_limit, clamp_limit)
    activated = ((up_val + 1.0) * gate_val * jax.nn.sigmoid(glu_alpha * gate_val)).astype(
        jnp.bfloat16
    )
    partials_t = lax.dot_general(
        expert_down[0], activated, (((0,), (1,)), ((), ())), preferred_element_type=jnp.float32
    )
    expert_out_t = lax.psum_scatter(
        partials_t.astype(jnp.bfloat16), "mp", scatter_dimension=0, tiled=True
    )
    local_width = expert_out_t.shape[0]
    expert_out = expert_out_t.T.reshape(expert_count, capacity, local_width)
    returned = lax.all_to_all(expert_out, "expert", split_axis=0, concat_axis=0, tiled=True)
    picked = returned.reshape(expert_count * capacity, local_width)[target].reshape(
        tok_count, top_count, local_width
    )
    moe_sum = jnp.sum(picked.astype(jnp.float32) * route_weights[0][..., None], axis=1)
    hidden = (first_out.astype(jnp.float32) + moe_sum).astype(jnp.bfloat16)
    return (hidden[None], key_rotary[None], value_fresh[None])


def solution(mesh):
    placed = (
        P("batch", "expert", "mp"),
        P("batch", None),
        P(),
        P("expert", "mp"),
        P("expert", "mp"),
        P("expert", "mp"),
        P("mp", "expert"),
        P("mp"),
        P(),
        P("expert", None, None, "mp"),
        P("expert", "mp", None),
        P("batch", "expert", None),
        P("batch", "expert", None),
    )
    return jax.shard_map(
        shards,
        mesh=mesh,
        in_specs=placed,
        out_specs=(
            P("batch", "expert", "mp"),
            P("batch", "expert", "mp"),
            P("batch", "expert", "mp"),
        ),
        check_vma=False,
    )
```

```python
import math

import jax
import jax.numpy as jnp
from jax import lax
from jax.sharding import PartitionSpec as P

HEAD_SIZE = 64


eps = 1e-05
rope_base = 150000.0
clamp_limit = 7.0
glu_alpha = 1.702


def rms_norm(row_block, gain):
    values = row_block.astype(jnp.float32)
    inv_scale = lax.rsqrt(jnp.mean(values * values, axis=-1, keepdims=True) + eps)
    return (values * inv_scale * gain).astype(jnp.bfloat16)


def apply_rotary(values, token_positions):
    half_dim = values.shape[-1] // 2
    inv_freq = jnp.power(
        rope_base, -2.0 * jnp.arange(half_dim, dtype=jnp.float32) / values.shape[-1]
    )
    rot_angle = token_positions.astype(jnp.float32)[:, None] * inv_freq[None, :]
    cosine = jnp.cos(rot_angle)[:, None, :]
    sine_val = jnp.sin(rot_angle)[:, None, :]
    first_half = values[..., :half_dim]
    second_half = values[..., half_dim:]
    return jnp.concatenate(
        [
            first_half * cosine - second_half * sine_val,
            second_half * cosine + first_half * sine_val,
        ],
        axis=-1,
    )


def gather_by_exchange(block, axis_name):
    count = lax.axis_size(axis_name)
    spread = jnp.broadcast_to(block[None], (count,) + block.shape)
    got = lax.all_to_all(spread, axis_name, split_axis=0, concat_axis=0, tiled=True)
    return got.reshape((count * block.shape[0],) + block.shape[1:])


def expert_rows(row_block, w_in, w_down):
    gate_val = jnp.dot(row_block, w_in[0], preferred_element_type=jnp.float32)
    up_val = jnp.dot(row_block, w_in[1], preferred_element_type=jnp.float32)
    gate_val = jnp.minimum(gate_val, clamp_limit)
    up_val = jnp.clip(up_val, -clamp_limit, clamp_limit)
    activated = ((up_val + 1.0) * gate_val * jax.nn.sigmoid(glu_alpha * gate_val)).astype(
        jnp.bfloat16
    )
    return jnp.dot(activated, w_down, preferred_element_type=jnp.float32)


def shards(
    tokens,
    segments,
    attn_gain,
    w_query,
    key_weight,
    value_weight,
    w_out,
    sink_head_logit,
    moe_gain,
    expert_in,
    expert_down,
    routes,
    route_weights,
):
    local_rows = tokens[0]
    tok_count = local_rows.shape[0]
    expert_devs = lax.axis_size("expert")
    row_start = lax.axis_index("expert") * tok_count
    mp_devs = lax.axis_size("mp")
    whole_rows = (
        gather_by_exchange(local_rows.T, "mp").reshape(-1, tok_count).T
    )
    input_normalised = rms_norm(whole_rows, attn_gain)
    query_cols = w_query.shape[1]
    kv_cols = key_weight.shape[1]
    big_weights = lax.all_gather(
        jnp.concatenate([w_query, w_out.T], axis=1), "expert", axis=0, tiled=True
    )
    query_weight = big_weights[:, :query_cols]
    out_weight_t = big_weights[:, query_cols:]
    kv_weight = gather_by_exchange(jnp.concatenate([key_weight, value_weight], axis=1), "expert")
    query_raw = jnp.dot(input_normalised, query_weight, preferred_element_type=jnp.float32)
    kv_raw = jnp.dot(input_normalised, kv_weight, preferred_element_type=jnp.float32)
    key_raw = kv_raw[:, :kv_cols]
    value_raw = kv_raw[:, kv_cols:]
    token_positions = row_start + jnp.arange(tok_count, dtype=jnp.int32)
    query_by_head = query_cols // HEAD_SIZE
    kv_heads = kv_cols // HEAD_SIZE
    heads_per_group = query_by_head // kv_heads
    query_matrix = apply_rotary(
        query_raw.reshape(tok_count, query_by_head, HEAD_SIZE), token_positions
    ).astype(jnp.bfloat16)
    key_rotary = (
        apply_rotary(key_raw.reshape(tok_count, kv_heads, HEAD_SIZE), token_positions)
        .astype(jnp.bfloat16)
        .reshape(tok_count, kv_cols)
    )
    value_fresh = value_raw.astype(jnp.bfloat16)
    kv_all = gather_by_exchange(jnp.concatenate([key_rotary, value_fresh], axis=1), "expert")
    keys_all = kv_all[:, :kv_cols]
    values_all = kv_all[:, kv_cols:]
    seq_len = keys_all.shape[0]
    seg_all = segments[0]
    seg_local = lax.dynamic_slice_in_dim(seg_all, row_start, tok_count)
    row_total = heads_per_group * tok_count
    query_rows = (
        query_matrix.reshape(tok_count, kv_heads, heads_per_group, HEAD_SIZE)
        .transpose(1, 2, 0, 3)
        .reshape(kv_heads, row_total, HEAD_SIZE)
    )
    key_by_head = keys_all.reshape(seq_len, kv_heads, HEAD_SIZE).transpose(1, 0, 2)
    value_by_head = values_all.reshape(seq_len, kv_heads, HEAD_SIZE).transpose(1, 0, 2)
    row_pos = jnp.tile(token_positions, heads_per_group)
    row_seg = jnp.tile(seg_local, heads_per_group)
    sink_rows = jnp.repeat(sink_head_logit.reshape(kv_heads, heads_per_group), tok_count, axis=1)
    key_block = math.gcd(seq_len, 512)
    block_count = seq_len // key_block
    score_scale = HEAD_SIZE ** (-0.5)

    def block_scores(index):
        key_first = index * key_block
        key_part = lax.dynamic_slice_in_dim(key_by_head, key_first, key_block, 1)
        scores = (
            jnp.einsum("hrd,hkd->hrk", query_rows, key_part, preferred_element_type=jnp.float32)
            * score_scale
        )
        key_pos = key_first + jnp.arange(key_block, dtype=jnp.int32)
        key_seg = lax.dynamic_slice_in_dim(seg_all, key_first, key_block, 0)
        allowed = (key_pos[None, :] <= row_pos[:, None]) & (key_seg[None, :] == row_seg[:, None])
        return jnp.where(allowed[None], scores, -jnp.inf)

    def max_step(index, running):
        return jnp.maximum(running, jnp.max(block_scores(index), axis=-1))

    row_max = lax.fori_loop(0, block_count, max_step, sink_rows)

    def sum_step(index, carried):
        weighted, denom = carried
        probs = jnp.exp(block_scores(index) - row_max[..., None]).astype(jnp.bfloat16)
        value_part = lax.dynamic_slice_in_dim(value_by_head, index * key_block, key_block, 1)
        weighted = weighted + jnp.einsum(
            "hrk,hkd->hrd", probs, value_part, preferred_element_type=jnp.float32
        )
        denom = denom + jnp.sum(probs, axis=-1, dtype=jnp.float32)
        return (weighted, denom)

    init_pair = (
        jnp.zeros((kv_heads, row_total, HEAD_SIZE), jnp.float32),
        jnp.zeros((kv_heads, row_total), jnp.float32),
    )
    weighted, denom = lax.fori_loop(0, block_count, sum_step, init_pair)
    denom = denom + jnp.exp(sink_rows - row_max)
    mixed = (weighted / denom[..., None]).astype(jnp.bfloat16)
    mixed = (
        mixed.reshape(kv_heads, heads_per_group, tok_count, HEAD_SIZE)
        .transpose(2, 0, 1, 3)
        .reshape(tok_count, query_cols)
    )
    out_terms = lax.dot_general(
        mixed, out_weight_t, (((1,), (1,)), ((), ())), preferred_element_type=jnp.float32
    )
    model_width = out_terms.shape[1]
    out_pieces = out_terms.astype(jnp.bfloat16).reshape(tok_count, mp_devs, model_width // mp_devs)
    out_got = lax.all_to_all(
        out_pieces.transpose(1, 0, 2), "mp", split_axis=0, concat_axis=0, tiled=True
    )
    attn_part = jnp.sum(out_got.astype(jnp.float32), axis=0)
    first_out = (local_rows.astype(jnp.float32) + attn_part).astype(jnp.bfloat16)
    top_count = routes.shape[2]
    local_experts = expert_in.shape[0]
    expert_count = local_experts * expert_devs
    capacity = 3 * tok_count * top_count // (2 * expert_count)
    chosen = routes[0].reshape(tok_count * top_count)
    onehot = (chosen[:, None] == jnp.arange(expert_count, dtype=jnp.int32)[None, :]).astype(
        jnp.int32
    )
    ranks = jnp.sum((jnp.cumsum(onehot, axis=0) - onehot) * onehot, axis=1)
    target = chosen * capacity + ranks
    source_row = (
        jnp.full((expert_count * capacity,), tok_count, jnp.int32)
        .at[target]
        .set(jnp.arange(tok_count * top_count, dtype=jnp.int32) // top_count)
    )
    padded = jnp.concatenate(
        [first_out, jnp.zeros((1, first_out.shape[1]), jnp.bfloat16)], axis=0
    )
    outgoing = padded[source_row].reshape(expert_count, capacity, padded.shape[1])
    arrived = lax.all_to_all(outgoing, "expert", split_axis=0, concat_axis=0, tiled=True)
    arrived_rows = arrived.reshape(expert_count * capacity, arrived.shape[2])
    inputs = rms_norm(lax.all_gather(arrived_rows, "mp", axis=1, tiled=True), moe_gain)
    w_in = expert_in[0]
    gate_val = jnp.dot(inputs, w_in[0], preferred_element_type=jnp.float32)
    up_val = jnp.dot(inputs, w_in[1], preferred_element_type=jnp.float32)
    gate_val = jnp.minimum(gate_val, clamp_limit)
    up_val = jnp.clip(up_val, -clamp_limit, clamp_limit)
    activated = ((up_val + 1.0) * gate_val * jax.nn.sigmoid(glu_alpha * gate_val)).astype(
        jnp.bfloat16
    )
    partials_t = lax.dot_general(
        expert_down[0], activated, (((0,), (1,)), ((), ())), preferred_element_type=jnp.float32
    )
    expert_out_t = lax.psum_scatter(
        partials_t.astype(jnp.bfloat16), "mp", scatter_dimension=0, tiled=True
    )
    local_width = expert_out_t.shape[0]
    expert_out = expert_out_t.T.reshape(expert_count, capacity, local_width)
    returned = lax.all_to_all(expert_out, "expert", split_axis=0, concat_axis=0, tiled=True)
    picked = returned.reshape(expert_count * capacity, local_width)[target].reshape(
        tok_count, top_count, local_width
    )
    moe_sum = jnp.sum(picked.astype(jnp.float32) * route_weights[0][..., None], axis=1)
    hidden = (first_out.astype(jnp.float32) + moe_sum).astype(jnp.bfloat16)
    return (hidden[None], key_rotary[None], value_fresh[None])


def solution(mesh):
    placed = (
        P("batch", "expert", "mp"),
        P("batch", None),
        P(),
        P("expert", "mp"),
        P("expert", "mp"),
        P("expert", "mp"),
        P("mp", "expert"),
        P("mp"),
        P(),
        P("expert", None, None, "mp"),
        P("expert", "mp", None),
        P("batch", "expert", None),
        P("batch", "expert", None),
    )
    return jax.shard_map(
        shards,
        mesh=mesh,
        in_specs=placed,
        out_specs=(
            P("batch", "expert", "mp"),
            P("batch", "expert", "mp"),
            P("batch", "expert", "mp"),
        ),
        check_vma=False,
    )
```

```python
import math

import jax
import jax.numpy as jnp
from jax import lax
from jax.sharding import PartitionSpec as P

HEAD_SIZE = 64


eps = 1e-05
rope_base = 150000.0
clamp_limit = 7.0
glu_alpha = 1.702


def rms_norm(row_block, gain):
    values = row_block.astype(jnp.float32)
    inv_scale = lax.rsqrt(jnp.mean(values * values, axis=-1, keepdims=True) + eps)
    return (values * inv_scale * gain).astype(jnp.bfloat16)


def apply_rotary(values, token_positions):
    half_dim = values.shape[-1] // 2
    inv_freq = jnp.power(
        rope_base, -2.0 * jnp.arange(half_dim, dtype=jnp.float32) / values.shape[-1]
    )
    rot_angle = token_positions.astype(jnp.float32)[:, None] * inv_freq[None, :]
    cosine = jnp.cos(rot_angle)[:, None, :]
    sine_val = jnp.sin(rot_angle)[:, None, :]
    first_half = values[..., :half_dim]
    second_half = values[..., half_dim:]
    return jnp.concatenate(
        [
            first_half * cosine - second_half * sine_val,
            second_half * cosine + first_half * sine_val,
        ],
        axis=-1,
    )


def gather_by_exchange(block, axis_name):
    count = lax.axis_size(axis_name)
    spread = jnp.broadcast_to(block[None], (count,) + block.shape)
    got = lax.all_to_all(spread, axis_name, split_axis=0, concat_axis=0, tiled=True)
    return got.reshape((count * block.shape[0],) + block.shape[1:])


def expert_rows(row_block, w_in, w_down):
    gate_val = jnp.dot(row_block, w_in[0], preferred_element_type=jnp.float32)
    up_val = jnp.dot(row_block, w_in[1], preferred_element_type=jnp.float32)
    gate_val = jnp.minimum(gate_val, clamp_limit)
    up_val = jnp.clip(up_val, -clamp_limit, clamp_limit)
    activated = ((up_val + 1.0) * gate_val * jax.nn.sigmoid(glu_alpha * gate_val)).astype(
        jnp.bfloat16
    )
    return jnp.dot(activated, w_down, preferred_element_type=jnp.float32)


def shards(
    tokens,
    segments,
    attn_gain,
    w_query,
    key_weight,
    value_weight,
    w_out,
    sink_head_logit,
    moe_gain,
    expert_in,
    expert_down,
    routes,
    route_weights,
):
    local_rows = tokens[0]
    tok_count = local_rows.shape[0]
    expert_devs = lax.axis_size("expert")
    row_start = lax.axis_index("expert") * tok_count
    mp_devs = lax.axis_size("mp")
    whole_rows = (
        gather_by_exchange(local_rows.T, "mp").reshape(-1, tok_count).T
    )
    input_normalised = rms_norm(whole_rows, attn_gain)
    query_cols = w_query.shape[1]
    kv_cols = key_weight.shape[1]
    big_weights = lax.all_gather(
        jnp.stack([w_query, w_out.T], axis=0), "expert", axis=1, tiled=True
    )
    query_weight = big_weights[0]
    out_weight_t = big_weights[1]
    kv_weight = gather_by_exchange(jnp.concatenate([key_weight, value_weight], axis=1), "expert")
    query_raw = jnp.dot(input_normalised, query_weight, preferred_element_type=jnp.float32)
    kv_raw = jnp.dot(input_normalised, kv_weight, preferred_element_type=jnp.float32)
    key_raw = kv_raw[:, :kv_cols]
    value_raw = kv_raw[:, kv_cols:]
    token_positions = row_start + jnp.arange(tok_count, dtype=jnp.int32)
    query_by_head = query_cols // HEAD_SIZE
    kv_heads = kv_cols // HEAD_SIZE
    heads_per_group = query_by_head // kv_heads
    query_matrix = apply_rotary(
        query_raw.reshape(tok_count, query_by_head, HEAD_SIZE), token_positions
    ).astype(jnp.bfloat16)
    key_rotary = (
        apply_rotary(key_raw.reshape(tok_count, kv_heads, HEAD_SIZE), token_positions)
        .astype(jnp.bfloat16)
        .reshape(tok_count, kv_cols)
    )
    value_fresh = value_raw.astype(jnp.bfloat16)
    kv_all = gather_by_exchange(jnp.concatenate([key_rotary, value_fresh], axis=1), "expert")
    keys_all = kv_all[:, :kv_cols]
    values_all = kv_all[:, kv_cols:]
    seq_len = keys_all.shape[0]
    seg_all = segments[0]
    seg_local = lax.dynamic_slice_in_dim(seg_all, row_start, tok_count)
    row_total = heads_per_group * tok_count
    query_rows = (
        query_matrix.reshape(tok_count, kv_heads, heads_per_group, HEAD_SIZE)
        .transpose(1, 2, 0, 3)
        .reshape(kv_heads, row_total, HEAD_SIZE)
    )
    key_by_head = keys_all.reshape(seq_len, kv_heads, HEAD_SIZE).transpose(1, 0, 2)
    value_by_head = values_all.reshape(seq_len, kv_heads, HEAD_SIZE).transpose(1, 0, 2)
    row_pos = jnp.tile(token_positions, heads_per_group)
    row_seg = jnp.tile(seg_local, heads_per_group)
    sink_rows = jnp.repeat(sink_head_logit.reshape(kv_heads, heads_per_group), tok_count, axis=1)
    key_block = math.gcd(seq_len, 512)
    block_count = seq_len // key_block
    score_scale = HEAD_SIZE ** (-0.5)

    def block_scores(index):
        key_first = index * key_block
        key_part = lax.dynamic_slice_in_dim(key_by_head, key_first, key_block, 1)
        scores = (
            jnp.einsum("hrd,hkd->hrk", query_rows, key_part, preferred_element_type=jnp.float32)
            * score_scale
        )
        key_pos = key_first + jnp.arange(key_block, dtype=jnp.int32)
        key_seg = lax.dynamic_slice_in_dim(seg_all, key_first, key_block, 0)
        allowed = (key_pos[None, :] <= row_pos[:, None]) & (key_seg[None, :] == row_seg[:, None])
        return jnp.where(allowed[None], scores, -jnp.inf)

    def max_step(index, running):
        return jnp.maximum(running, jnp.max(block_scores(index), axis=-1))

    row_max = lax.fori_loop(0, block_count, max_step, sink_rows)

    def sum_step(index, carried):
        weighted, denom = carried
        probs = jnp.exp(block_scores(index) - row_max[..., None]).astype(jnp.bfloat16)
        value_part = lax.dynamic_slice_in_dim(value_by_head, index * key_block, key_block, 1)
        weighted = weighted + jnp.einsum(
            "hrk,hkd->hrd", probs, value_part, preferred_element_type=jnp.float32
        )
        denom = denom + jnp.sum(probs, axis=-1, dtype=jnp.float32)
        return (weighted, denom)

    init_pair = (
        jnp.zeros((kv_heads, row_total, HEAD_SIZE), jnp.float32),
        jnp.zeros((kv_heads, row_total), jnp.float32),
    )
    weighted, denom = lax.fori_loop(0, block_count, sum_step, init_pair)
    denom = denom + jnp.exp(sink_rows - row_max)
    mixed = (weighted / denom[..., None]).astype(jnp.bfloat16)
    mixed = (
        mixed.reshape(kv_heads, heads_per_group, tok_count, HEAD_SIZE)
        .transpose(2, 0, 1, 3)
        .reshape(tok_count, query_cols)
    )
    out_terms = lax.dot_general(
        mixed, out_weight_t, (((1,), (1,)), ((), ())), preferred_element_type=jnp.float32
    )
    model_width = out_terms.shape[1]
    out_pieces = out_terms.astype(jnp.bfloat16).reshape(tok_count, mp_devs, model_width // mp_devs)
    out_got = lax.all_to_all(
        out_pieces.transpose(1, 0, 2), "mp", split_axis=0, concat_axis=0, tiled=True
    )
    attn_part = jnp.sum(out_got.astype(jnp.float32), axis=0)
    first_out = (local_rows.astype(jnp.float32) + attn_part).astype(jnp.bfloat16)
    top_count = routes.shape[2]
    local_experts = expert_in.shape[0]
    expert_count = local_experts * expert_devs
    capacity = 3 * tok_count * top_count // (2 * expert_count)
    chosen = routes[0].reshape(tok_count * top_count)
    onehot = (chosen[:, None] == jnp.arange(expert_count, dtype=jnp.int32)[None, :]).astype(
        jnp.int32
    )
    ranks = jnp.sum((jnp.cumsum(onehot, axis=0) - onehot) * onehot, axis=1)
    target = chosen * capacity + ranks
    source_row = (
        jnp.full((expert_count * capacity,), tok_count, jnp.int32)
        .at[target]
        .set(jnp.arange(tok_count * top_count, dtype=jnp.int32) // top_count)
    )
    padded = jnp.concatenate(
        [first_out, jnp.zeros((1, first_out.shape[1]), jnp.bfloat16)], axis=0
    )
    local_cols = padded.shape[1]
    outgoing = padded[source_row].reshape(expert_count, capacity, local_cols)
    arrived = lax.all_to_all(outgoing, "expert", split_axis=0, concat_axis=0, tiled=True)
    arrived_rows = arrived.reshape(expert_count * capacity, local_cols)
    inputs = rms_norm(lax.all_gather(arrived_rows, "mp", axis=1, tiled=True), moe_gain)
    w_in = expert_in[0]
    gate_val = jnp.dot(inputs, w_in[0], preferred_element_type=jnp.float32)
    up_val = jnp.dot(inputs, w_in[1], preferred_element_type=jnp.float32)
    gate_val = jnp.minimum(gate_val, clamp_limit)
    up_val = jnp.clip(up_val, -clamp_limit, clamp_limit)
    activated = ((up_val + 1.0) * gate_val * jax.nn.sigmoid(glu_alpha * gate_val)).astype(
        jnp.bfloat16
    )
    partials_t = lax.dot_general(
        expert_down[0], activated, (((0,), (1,)), ((), ())), preferred_element_type=jnp.float32
    )
    local_width = model_width // mp_devs
    partial_pieces = partials_t.astype(jnp.bfloat16).reshape(mp_devs, local_width, -1)
    expert_out_t = jnp.sum(
        lax.all_to_all(partial_pieces, "mp", split_axis=0, concat_axis=0, tiled=True).astype(
            jnp.float32
        ),
        axis=0,
    ).astype(jnp.bfloat16)
    expert_out = expert_out_t.T.reshape(expert_count, capacity, local_width)
    returned = lax.all_to_all(expert_out, "expert", split_axis=0, concat_axis=0, tiled=True)
    picked = returned.reshape(expert_count * capacity, local_width)[target].reshape(
        tok_count, top_count, local_width
    )
    moe_sum = jnp.sum(picked.astype(jnp.float32) * route_weights[0][..., None], axis=1)
    hidden = (first_out.astype(jnp.float32) + moe_sum).astype(jnp.bfloat16)
    return (hidden[None], key_rotary[None], value_fresh[None])


def solution(mesh):
    placed = (
        P("batch", "expert", "mp"),
        P("batch", None),
        P(),
        P("expert", "mp"),
        P("expert", "mp"),
        P("expert", "mp"),
        P("mp", "expert"),
        P("mp"),
        P(),
        P("expert", None, None, "mp"),
        P("expert", "mp", None),
        P("batch", "expert", None),
        P("batch", "expert", None),
    )
    return jax.shard_map(
        shards,
        mesh=mesh,
        in_specs=placed,
        out_specs=(
            P("batch", "expert", "mp"),
            P("batch", "expert", "mp"),
            P("batch", "expert", "mp"),
        ),
        check_vma=False,
    )
```

```python
import math

import jax
import jax.numpy as jnp
from jax import lax
from jax.sharding import PartitionSpec as P

HEAD_SIZE = 64


eps = 1e-05
rope_base = 150000.0
clamp_limit = 7.0
glu_alpha = 1.702


def rms_norm(row_block, gain):
    values = row_block.astype(jnp.float32)
    inv_scale = lax.rsqrt(jnp.mean(values * values, axis=-1, keepdims=True) + eps)
    return (values * inv_scale * gain).astype(jnp.bfloat16)


def apply_rotary(values, token_positions):
    half_dim = values.shape[-1] // 2
    inv_freq = jnp.power(
        rope_base, -2.0 * jnp.arange(half_dim, dtype=jnp.float32) / values.shape[-1]
    )
    rot_angle = token_positions.astype(jnp.float32)[:, None] * inv_freq[None, :]
    cosine = jnp.cos(rot_angle)[:, None, :]
    sine_val = jnp.sin(rot_angle)[:, None, :]
    first_half = values[..., :half_dim]
    second_half = values[..., half_dim:]
    return jnp.concatenate(
        [
            first_half * cosine - second_half * sine_val,
            second_half * cosine + first_half * sine_val,
        ],
        axis=-1,
    )


def gather_by_exchange(block, axis_name):
    count = lax.axis_size(axis_name)
    spread = jnp.broadcast_to(block[None], (count,) + block.shape)
    got = lax.all_to_all(spread, axis_name, split_axis=0, concat_axis=0, tiled=True)
    return got.reshape((count * block.shape[0],) + block.shape[1:])


def expert_rows(row_block, w_in, w_down):
    gate_val = jnp.dot(row_block, w_in[0], preferred_element_type=jnp.float32)
    up_val = jnp.dot(row_block, w_in[1], preferred_element_type=jnp.float32)
    gate_val = jnp.minimum(gate_val, clamp_limit)
    up_val = jnp.clip(up_val, -clamp_limit, clamp_limit)
    activated = ((up_val + 1.0) * gate_val * jax.nn.sigmoid(glu_alpha * gate_val)).astype(
        jnp.bfloat16
    )
    return jnp.dot(activated, w_down, preferred_element_type=jnp.float32)


def shards(
    tokens,
    segments,
    attn_gain,
    w_query,
    key_weight,
    value_weight,
    w_out,
    sink_head_logit,
    moe_gain,
    expert_in,
    expert_down,
    routes,
    route_weights,
):
    local_rows = tokens[0]
    tok_count = local_rows.shape[0]
    expert_devs = lax.axis_size("expert")
    row_start = lax.axis_index("expert") * tok_count
    mp_devs = lax.axis_size("mp")
    whole_rows = (
        gather_by_exchange(local_rows.T, "mp").reshape(-1, tok_count).T
    )
    input_normalised = rms_norm(whole_rows, attn_gain)
    query_cols = w_query.shape[1]
    kv_cols = key_weight.shape[1]
    big_weights = lax.all_gather(
        jnp.concatenate([w_query, w_out.T], axis=1), "expert", axis=0, tiled=True
    )
    query_weight = big_weights[:, :query_cols]
    out_weight_t = big_weights[:, query_cols:]
    kv_weight = gather_by_exchange(jnp.concatenate([key_weight, value_weight], axis=1), "expert")
    query_raw = jnp.dot(input_normalised, query_weight, preferred_element_type=jnp.float32)
    kv_raw = jnp.dot(input_normalised, kv_weight, preferred_element_type=jnp.float32)
    key_raw = kv_raw[:, :kv_cols]
    value_raw = kv_raw[:, kv_cols:]
    token_positions = row_start + jnp.arange(tok_count, dtype=jnp.int32)
    query_by_head = query_cols // HEAD_SIZE
    kv_heads = kv_cols // HEAD_SIZE
    heads_per_group = query_by_head // kv_heads
    query_matrix = apply_rotary(
        query_raw.reshape(tok_count, query_by_head, HEAD_SIZE), token_positions
    ).astype(jnp.bfloat16)
    key_rotary = (
        apply_rotary(key_raw.reshape(tok_count, kv_heads, HEAD_SIZE), token_positions)
        .astype(jnp.bfloat16)
        .reshape(tok_count, kv_cols)
    )
    value_fresh = value_raw.astype(jnp.bfloat16)
    kv_all = gather_by_exchange(jnp.concatenate([key_rotary, value_fresh], axis=1), "expert")
    keys_all = kv_all[:, :kv_cols]
    values_all = kv_all[:, kv_cols:]
    seq_len = keys_all.shape[0]
    seg_all = segments[0]
    seg_local = lax.dynamic_slice_in_dim(seg_all, row_start, tok_count)
    row_total = heads_per_group * tok_count
    query_rows = (
        query_matrix.reshape(tok_count, kv_heads, heads_per_group, HEAD_SIZE)
        .transpose(1, 2, 0, 3)
        .reshape(kv_heads, row_total, HEAD_SIZE)
    )
    key_by_head = keys_all.reshape(seq_len, kv_heads, HEAD_SIZE).transpose(1, 0, 2)
    value_by_head = values_all.reshape(seq_len, kv_heads, HEAD_SIZE).transpose(1, 0, 2)
    row_pos = jnp.tile(token_positions, heads_per_group)
    row_seg = jnp.tile(seg_local, heads_per_group)
    sink_rows = jnp.repeat(sink_head_logit.reshape(kv_heads, heads_per_group), tok_count, axis=1)
    key_block = math.gcd(seq_len, 512)
    block_count = seq_len // key_block
    score_scale = HEAD_SIZE ** (-0.5)

    def block_scores(index):
        key_first = index * key_block
        key_part = lax.dynamic_slice_in_dim(key_by_head, key_first, key_block, 1)
        scores = (
            jnp.einsum("hrd,hkd->hrk", query_rows, key_part, preferred_element_type=jnp.float32)
            * score_scale
        )
        key_pos = key_first + jnp.arange(key_block, dtype=jnp.int32)
        key_seg = lax.dynamic_slice_in_dim(seg_all, key_first, key_block, 0)
        allowed = (key_pos[None, :] <= row_pos[:, None]) & (key_seg[None, :] == row_seg[:, None])
        return jnp.where(allowed[None], scores, -jnp.inf)

    def max_step(index, running):
        return jnp.maximum(running, jnp.max(block_scores(index), axis=-1))

    row_max = lax.fori_loop(0, block_count, max_step, sink_rows)

    def sum_step(index, carried):
        weighted, denom = carried
        probs = jnp.exp(block_scores(index) - row_max[..., None]).astype(jnp.bfloat16)
        value_part = lax.dynamic_slice_in_dim(value_by_head, index * key_block, key_block, 1)
        weighted = weighted + jnp.einsum(
            "hrk,hkd->hrd", probs, value_part, preferred_element_type=jnp.float32
        )
        denom = denom + jnp.sum(probs, axis=-1, dtype=jnp.float32)
        return (weighted, denom)

    init_pair = (
        jnp.zeros((kv_heads, row_total, HEAD_SIZE), jnp.float32),
        jnp.zeros((kv_heads, row_total), jnp.float32),
    )
    weighted, denom = lax.fori_loop(0, block_count, sum_step, init_pair)
    denom = denom + jnp.exp(sink_rows - row_max)
    mixed = (weighted / denom[..., None]).astype(jnp.bfloat16)
    mixed = (
        mixed.reshape(kv_heads, heads_per_group, tok_count, HEAD_SIZE)
        .transpose(2, 0, 1, 3)
        .reshape(tok_count, query_cols)
    )
    out_terms = lax.dot_general(
        mixed, out_weight_t, (((1,), (1,)), ((), ())), preferred_element_type=jnp.float32
    )
    model_width = out_terms.shape[1]
    out_pieces = out_terms.astype(jnp.bfloat16).reshape(tok_count, mp_devs, model_width // mp_devs)
    out_got = lax.all_to_all(
        out_pieces.transpose(1, 0, 2), "mp", split_axis=0, concat_axis=0, tiled=True
    )
    attn_part = jnp.sum(out_got.astype(jnp.float32), axis=0)
    first_out = (local_rows.astype(jnp.float32) + attn_part).astype(jnp.bfloat16)
    top_count = routes.shape[2]
    local_experts = expert_in.shape[0]
    expert_count = local_experts * expert_devs
    capacity = 3 * tok_count * top_count // (2 * expert_count)
    chosen = routes[0].reshape(tok_count * top_count)
    onehot = (chosen[:, None] == jnp.arange(expert_count, dtype=jnp.int32)[None, :]).astype(
        jnp.int32
    )
    ranks = jnp.sum((jnp.cumsum(onehot, axis=0) - onehot) * onehot, axis=1)
    target = chosen * capacity + ranks
    source_row = (
        jnp.full((expert_count * capacity,), tok_count, jnp.int32)
        .at[target]
        .set(jnp.arange(tok_count * top_count, dtype=jnp.int32) // top_count)
    )
    padded = jnp.concatenate(
        [first_out, jnp.zeros((1, first_out.shape[1]), jnp.bfloat16)], axis=0
    )
    outgoing = padded[source_row].reshape(expert_count, capacity, padded.shape[1])
    arrived = lax.all_to_all(outgoing, "expert", split_axis=0, concat_axis=0, tiled=True)
    arrived_rows = arrived.reshape(expert_count * capacity, arrived.shape[2])
    sc_rows = 256
    rows_by_sc = lax.all_gather(arrived_rows[:sc_rows], "mp", axis=1, tiled=True)
    rows_by_exchange = gather_by_exchange(arrived_rows[sc_rows:].T, "mp").T
    inputs = rms_norm(jnp.concatenate([rows_by_sc, rows_by_exchange], axis=0), moe_gain)
    w_in = expert_in[0]
    gate_val = jnp.dot(inputs, w_in[0], preferred_element_type=jnp.float32)
    up_val = jnp.dot(inputs, w_in[1], preferred_element_type=jnp.float32)
    gate_val = jnp.minimum(gate_val, clamp_limit)
    up_val = jnp.clip(up_val, -clamp_limit, clamp_limit)
    activated = ((up_val + 1.0) * gate_val * jax.nn.sigmoid(glu_alpha * gate_val)).astype(
        jnp.bfloat16
    )
    partials_t = lax.dot_general(
        expert_down[0], activated, (((0,), (1,)), ((), ())), preferred_element_type=jnp.float32
    )
    partials_bf = partials_t.astype(jnp.bfloat16)
    local_width = partials_bf.shape[0] // mp_devs
    out_by_sc = lax.psum_scatter(
        partials_bf[:, :sc_rows], "mp", scatter_dimension=0, tiled=True
    )
    out_by_exchange = jnp.sum(
        lax.all_to_all(
            partials_bf[:, sc_rows:].reshape(mp_devs, local_width, -1),
            "mp",
            split_axis=0,
            concat_axis=0,
            tiled=True,
        ).astype(jnp.float32),
        axis=0,
    ).astype(jnp.bfloat16)
    expert_out_t = jnp.concatenate([out_by_sc, out_by_exchange], axis=1)
    expert_out = expert_out_t.T.reshape(expert_count, capacity, local_width)
    returned = lax.all_to_all(expert_out, "expert", split_axis=0, concat_axis=0, tiled=True)
    picked = returned.reshape(expert_count * capacity, local_width)[target].reshape(
        tok_count, top_count, local_width
    )
    moe_sum = jnp.sum(picked.astype(jnp.float32) * route_weights[0][..., None], axis=1)
    hidden = (first_out.astype(jnp.float32) + moe_sum).astype(jnp.bfloat16)
    return (hidden[None], key_rotary[None], value_fresh[None])


def solution(mesh):
    placed = (
        P("batch", "expert", "mp"),
        P("batch", None),
        P(),
        P("expert", "mp"),
        P("expert", "mp"),
        P("expert", "mp"),
        P("mp", "expert"),
        P("mp"),
        P(),
        P("expert", None, None, "mp"),
        P("expert", "mp", None),
        P("batch", "expert", None),
        P("batch", "expert", None),
    )
    return jax.shard_map(
        shards,
        mesh=mesh,
        in_specs=placed,
        out_specs=(
            P("batch", "expert", "mp"),
            P("batch", "expert", "mp"),
            P("batch", "expert", "mp"),
        ),
        check_vma=False,
    )
```

```python
import math

import jax
import jax.numpy as jnp
from jax import lax
from jax.sharding import PartitionSpec as P

HEAD_SIZE = 64


eps = 1e-05
rope_base = 150000.0
clamp_limit = 7.0
glu_alpha = 1.702


def rms_norm(row_block, gain):
    values = row_block.astype(jnp.float32)
    inv_scale = lax.rsqrt(jnp.mean(values * values, axis=-1, keepdims=True) + eps)
    return (values * inv_scale * gain).astype(jnp.bfloat16)


def apply_rotary(values, token_positions):
    half_dim = values.shape[-1] // 2
    inv_freq = jnp.power(
        rope_base, -2.0 * jnp.arange(half_dim, dtype=jnp.float32) / values.shape[-1]
    )
    rot_angle = token_positions.astype(jnp.float32)[:, None] * inv_freq[None, :]
    cosine = jnp.cos(rot_angle)[:, None, :]
    sine_val = jnp.sin(rot_angle)[:, None, :]
    first_half = values[..., :half_dim]
    second_half = values[..., half_dim:]
    return jnp.concatenate(
        [
            first_half * cosine - second_half * sine_val,
            second_half * cosine + first_half * sine_val,
        ],
        axis=-1,
    )


def gather_by_exchange(block, axis_name):
    count = lax.axis_size(axis_name)
    spread = jnp.broadcast_to(block[None], (count,) + block.shape)
    got = lax.all_to_all(spread, axis_name, split_axis=0, concat_axis=0, tiled=True)
    return got.reshape((count * block.shape[0],) + block.shape[1:])


def expert_rows(row_block, w_in, w_down):
    gate_val = jnp.dot(row_block, w_in[0], preferred_element_type=jnp.float32)
    up_val = jnp.dot(row_block, w_in[1], preferred_element_type=jnp.float32)
    gate_val = jnp.minimum(gate_val, clamp_limit)
    up_val = jnp.clip(up_val, -clamp_limit, clamp_limit)
    activated = ((up_val + 1.0) * gate_val * jax.nn.sigmoid(glu_alpha * gate_val)).astype(
        jnp.bfloat16
    )
    return jnp.dot(activated, w_down, preferred_element_type=jnp.float32)


def shards(
    tokens,
    segments,
    attn_gain,
    w_query,
    key_weight,
    value_weight,
    w_out,
    sink_head_logit,
    moe_gain,
    expert_in,
    expert_down,
    routes,
    route_weights,
):
    local_rows = tokens[0]
    tok_count = local_rows.shape[0]
    expert_devs = lax.axis_size("expert")
    row_start = lax.axis_index("expert") * tok_count
    mp_devs = lax.axis_size("mp")
    whole_rows = (
        gather_by_exchange(local_rows.T, "mp").reshape(-1, tok_count).T
    )
    input_normalised = rms_norm(whole_rows, attn_gain)
    query_cols = w_query.shape[1]
    kv_cols = key_weight.shape[1]
    big_weights = lax.all_gather(jnp.concatenate([w_query, w_out.T], axis=1), "expert", axis=0)
    query_weight = big_weights[:, :, :query_cols]
    out_weight_t = big_weights[:, :, query_cols:]
    kv_weight = gather_by_exchange(jnp.concatenate([key_weight, value_weight], axis=1), "expert")
    query_raw = jnp.einsum(
        "tef,efc->tc",
        input_normalised.reshape(tok_count, expert_devs, -1),
        query_weight,
        preferred_element_type=jnp.float32,
    )
    kv_raw = jnp.dot(input_normalised, kv_weight, preferred_element_type=jnp.float32)
    key_raw = kv_raw[:, :kv_cols]
    value_raw = kv_raw[:, kv_cols:]
    token_positions = row_start + jnp.arange(tok_count, dtype=jnp.int32)
    query_by_head = query_cols // HEAD_SIZE
    kv_heads = kv_cols // HEAD_SIZE
    heads_per_group = query_by_head // kv_heads
    query_matrix = apply_rotary(
        query_raw.reshape(tok_count, query_by_head, HEAD_SIZE), token_positions
    ).astype(jnp.bfloat16)
    key_rotary = (
        apply_rotary(key_raw.reshape(tok_count, kv_heads, HEAD_SIZE), token_positions)
        .astype(jnp.bfloat16)
        .reshape(tok_count, kv_cols)
    )
    value_fresh = value_raw.astype(jnp.bfloat16)
    kv_all = gather_by_exchange(jnp.concatenate([key_rotary, value_fresh], axis=1), "expert")
    keys_all = kv_all[:, :kv_cols]
    values_all = kv_all[:, kv_cols:]
    seq_len = keys_all.shape[0]
    seg_all = segments[0]
    seg_local = lax.dynamic_slice_in_dim(seg_all, row_start, tok_count)
    row_total = heads_per_group * tok_count
    query_rows = (
        query_matrix.reshape(tok_count, kv_heads, heads_per_group, HEAD_SIZE)
        .transpose(1, 2, 0, 3)
        .reshape(kv_heads, row_total, HEAD_SIZE)
    )
    key_by_head = keys_all.reshape(seq_len, kv_heads, HEAD_SIZE).transpose(1, 0, 2)
    value_by_head = values_all.reshape(seq_len, kv_heads, HEAD_SIZE).transpose(1, 0, 2)
    row_pos = jnp.tile(token_positions, heads_per_group)
    row_seg = jnp.tile(seg_local, heads_per_group)
    sink_rows = jnp.repeat(sink_head_logit.reshape(kv_heads, heads_per_group), tok_count, axis=1)
    key_block = math.gcd(seq_len, 512)
    block_count = seq_len // key_block
    score_scale = HEAD_SIZE ** (-0.5)

    def block_scores(index):
        key_first = index * key_block
        key_part = lax.dynamic_slice_in_dim(key_by_head, key_first, key_block, 1)
        scores = (
            jnp.einsum("hrd,hkd->hrk", query_rows, key_part, preferred_element_type=jnp.float32)
            * score_scale
        )
        key_pos = key_first + jnp.arange(key_block, dtype=jnp.int32)
        key_seg = lax.dynamic_slice_in_dim(seg_all, key_first, key_block, 0)
        allowed = (key_pos[None, :] <= row_pos[:, None]) & (key_seg[None, :] == row_seg[:, None])
        return jnp.where(allowed[None], scores, -jnp.inf)

    def max_step(index, running):
        return jnp.maximum(running, jnp.max(block_scores(index), axis=-1))

    row_max = lax.fori_loop(0, block_count, max_step, sink_rows)

    def sum_step(index, carried):
        weighted, denom = carried
        probs = jnp.exp(block_scores(index) - row_max[..., None]).astype(jnp.bfloat16)
        value_part = lax.dynamic_slice_in_dim(value_by_head, index * key_block, key_block, 1)
        weighted = weighted + jnp.einsum(
            "hrk,hkd->hrd", probs, value_part, preferred_element_type=jnp.float32
        )
        denom = denom + jnp.sum(probs, axis=-1, dtype=jnp.float32)
        return (weighted, denom)

    init_pair = (
        jnp.zeros((kv_heads, row_total, HEAD_SIZE), jnp.float32),
        jnp.zeros((kv_heads, row_total), jnp.float32),
    )
    weighted, denom = lax.fori_loop(0, block_count, sum_step, init_pair)
    denom = denom + jnp.exp(sink_rows - row_max)
    mixed = (weighted / denom[..., None]).astype(jnp.bfloat16)
    mixed = (
        mixed.reshape(kv_heads, heads_per_group, tok_count, HEAD_SIZE)
        .transpose(2, 0, 1, 3)
        .reshape(tok_count, query_cols)
    )
    out_terms = jnp.einsum(
        "tc,efc->tef", mixed, out_weight_t, preferred_element_type=jnp.float32
    ).reshape(tok_count, -1)
    model_width = out_terms.shape[1]
    out_pieces = out_terms.astype(jnp.bfloat16).reshape(tok_count, mp_devs, model_width // mp_devs)
    out_got = lax.all_to_all(
        out_pieces.transpose(1, 0, 2), "mp", split_axis=0, concat_axis=0, tiled=True
    )
    attn_part = jnp.sum(out_got.astype(jnp.float32), axis=0)
    first_out = (local_rows.astype(jnp.float32) + attn_part).astype(jnp.bfloat16)
    top_count = routes.shape[2]
    local_experts = expert_in.shape[0]
    expert_count = local_experts * expert_devs
    capacity = 3 * tok_count * top_count // (2 * expert_count)
    chosen = routes[0].reshape(tok_count * top_count)
    onehot = (chosen[:, None] == jnp.arange(expert_count, dtype=jnp.int32)[None, :]).astype(
        jnp.int32
    )
    ranks = jnp.sum((jnp.cumsum(onehot, axis=0) - onehot) * onehot, axis=1)
    target = chosen * capacity + ranks
    source_row = (
        jnp.full((expert_count * capacity,), tok_count, jnp.int32)
        .at[target]
        .set(jnp.arange(tok_count * top_count, dtype=jnp.int32) // top_count)
    )
    padded = jnp.concatenate(
        [first_out, jnp.zeros((1, first_out.shape[1]), jnp.bfloat16)], axis=0
    )
    outgoing = padded[source_row].reshape(expert_count, capacity, padded.shape[1])
    arrived = lax.all_to_all(outgoing, "expert", split_axis=0, concat_axis=0, tiled=True)
    arrived_rows = arrived.reshape(expert_count * capacity, arrived.shape[2])
    inputs = rms_norm(lax.all_gather(arrived_rows, "mp", axis=1, tiled=True), moe_gain)
    w_in = expert_in[0]
    gate_val = jnp.dot(inputs, w_in[0], preferred_element_type=jnp.float32)
    up_val = jnp.dot(inputs, w_in[1], preferred_element_type=jnp.float32)
    gate_val = jnp.minimum(gate_val, clamp_limit)
    up_val = jnp.clip(up_val, -clamp_limit, clamp_limit)
    activated = ((up_val + 1.0) * gate_val * jax.nn.sigmoid(glu_alpha * gate_val)).astype(
        jnp.bfloat16
    )
    partials = jnp.einsum(
        "rh,hjf->jrf",
        activated,
        expert_down[0].reshape(expert_down.shape[1], mp_devs, -1),
        preferred_element_type=jnp.float32,
    )
    expert_out = lax.psum_scatter(
        partials.astype(jnp.bfloat16), "mp", scatter_dimension=0, tiled=True
    ).reshape(expert_count, capacity, -1)
    local_width = expert_out.shape[2]
    returned = lax.all_to_all(expert_out, "expert", split_axis=0, concat_axis=0, tiled=True)
    picked = returned.reshape(expert_count * capacity, local_width)[target].reshape(
        tok_count, top_count, local_width
    )
    moe_sum = jnp.sum(picked.astype(jnp.float32) * route_weights[0][..., None], axis=1)
    hidden = (first_out.astype(jnp.float32) + moe_sum).astype(jnp.bfloat16)
    return (hidden[None], key_rotary[None], value_fresh[None])


def solution(mesh):
    placed = (
        P("batch", "expert", "mp"),
        P("batch", None),
        P(),
        P("expert", "mp"),
        P("expert", "mp"),
        P("expert", "mp"),
        P("mp", "expert"),
        P("mp"),
        P(),
        P("expert", None, None, "mp"),
        P("expert", "mp", None),
        P("batch", "expert", None),
        P("batch", "expert", None),
    )
    return jax.shard_map(
        shards,
        mesh=mesh,
        in_specs=placed,
        out_specs=(
            P("batch", "expert", "mp"),
            P("batch", "expert", "mp"),
            P("batch", "expert", "mp"),
        ),
        check_vma=False,
    )
```

```python
import math

import jax
import jax.numpy as jnp
from jax import lax
from jax.sharding import PartitionSpec as P

HEAD_SIZE = 64


eps = 1e-05
rope_base = 150000.0
clamp_limit = 7.0
glu_alpha = 1.702


def rms_norm(row_block, gain):
    values = row_block.astype(jnp.float32)
    inv_scale = lax.rsqrt(jnp.mean(values * values, axis=-1, keepdims=True) + eps)
    return (values * inv_scale * gain).astype(jnp.bfloat16)


def apply_rotary(values, token_positions):
    half_dim = values.shape[-1] // 2
    inv_freq = jnp.power(
        rope_base, -2.0 * jnp.arange(half_dim, dtype=jnp.float32) / values.shape[-1]
    )
    rot_angle = token_positions.astype(jnp.float32)[:, None] * inv_freq[None, :]
    cosine = jnp.cos(rot_angle)[:, None, :]
    sine_val = jnp.sin(rot_angle)[:, None, :]
    first_half = values[..., :half_dim]
    second_half = values[..., half_dim:]
    return jnp.concatenate(
        [
            first_half * cosine - second_half * sine_val,
            second_half * cosine + first_half * sine_val,
        ],
        axis=-1,
    )


def gather_by_exchange(block, axis_name):
    count = lax.axis_size(axis_name)
    spread = jnp.broadcast_to(block[None], (count,) + block.shape)
    got = lax.all_to_all(spread, axis_name, split_axis=0, concat_axis=0, tiled=True)
    return got.reshape((count * block.shape[0],) + block.shape[1:])


def expert_rows(row_block, w_in, w_down):
    gate_val = jnp.dot(row_block, w_in[0], preferred_element_type=jnp.float32)
    up_val = jnp.dot(row_block, w_in[1], preferred_element_type=jnp.float32)
    gate_val = jnp.minimum(gate_val, clamp_limit)
    up_val = jnp.clip(up_val, -clamp_limit, clamp_limit)
    activated = ((up_val + 1.0) * gate_val * jax.nn.sigmoid(glu_alpha * gate_val)).astype(
        jnp.bfloat16
    )
    return jnp.dot(activated, w_down, preferred_element_type=jnp.float32)


def shards(
    tokens,
    segments,
    attn_gain,
    w_query,
    key_weight,
    value_weight,
    w_out,
    sink_head_logit,
    moe_gain,
    expert_in,
    expert_down,
    routes,
    route_weights,
):
    local_rows = tokens[0]
    tok_count = local_rows.shape[0]
    expert_devs = lax.axis_size("expert")
    row_start = lax.axis_index("expert") * tok_count
    mp_devs = lax.axis_size("mp")
    whole_rows = (
        gather_by_exchange(local_rows.T, "mp").reshape(-1, tok_count).T
    )
    input_normalised = rms_norm(whole_rows, attn_gain)
    query_cols = w_query.shape[1]
    kv_cols = key_weight.shape[1]
    out_split = w_out.shape[0] // 2
    out_t = w_out.T
    big_weights = lax.all_gather(
        jnp.concatenate([w_query, out_t[:, :out_split]], axis=1), "expert", axis=0
    )
    query_weight = big_weights[:, :, :query_cols]
    out_weight_first = big_weights[:, :, query_cols:]
    out_weight_second = gather_by_exchange(out_t[:, out_split:], "expert").reshape(
        expert_devs, -1, w_out.shape[0] - out_split
    )
    kv_weight = gather_by_exchange(jnp.concatenate([key_weight, value_weight], axis=1), "expert")
    query_raw = jnp.einsum(
        "tef,efc->tc",
        input_normalised.reshape(tok_count, expert_devs, -1),
        query_weight,
        preferred_element_type=jnp.float32,
    )
    kv_raw = jnp.dot(input_normalised, kv_weight, preferred_element_type=jnp.float32)
    key_raw = kv_raw[:, :kv_cols]
    value_raw = kv_raw[:, kv_cols:]
    token_positions = row_start + jnp.arange(tok_count, dtype=jnp.int32)
    query_by_head = query_cols // HEAD_SIZE
    kv_heads = kv_cols // HEAD_SIZE
    heads_per_group = query_by_head // kv_heads
    query_matrix = apply_rotary(
        query_raw.reshape(tok_count, query_by_head, HEAD_SIZE), token_positions
    ).astype(jnp.bfloat16)
    key_rotary = (
        apply_rotary(key_raw.reshape(tok_count, kv_heads, HEAD_SIZE), token_positions)
        .astype(jnp.bfloat16)
        .reshape(tok_count, kv_cols)
    )
    value_fresh = value_raw.astype(jnp.bfloat16)
    kv_all = gather_by_exchange(jnp.concatenate([key_rotary, value_fresh], axis=1), "expert")
    keys_all = kv_all[:, :kv_cols]
    values_all = kv_all[:, kv_cols:]
    seq_len = keys_all.shape[0]
    seg_all = segments[0]
    seg_local = lax.dynamic_slice_in_dim(seg_all, row_start, tok_count)
    row_total = heads_per_group * tok_count
    query_rows = (
        query_matrix.reshape(tok_count, kv_heads, heads_per_group, HEAD_SIZE)
        .transpose(1, 2, 0, 3)
        .reshape(kv_heads, row_total, HEAD_SIZE)
    )
    key_by_head = keys_all.reshape(seq_len, kv_heads, HEAD_SIZE).transpose(1, 0, 2)
    value_by_head = values_all.reshape(seq_len, kv_heads, HEAD_SIZE).transpose(1, 0, 2)
    row_pos = jnp.tile(token_positions, heads_per_group)
    row_seg = jnp.tile(seg_local, heads_per_group)
    sink_rows = jnp.repeat(sink_head_logit.reshape(kv_heads, heads_per_group), tok_count, axis=1)
    key_block = math.gcd(seq_len, 512)
    block_count = seq_len // key_block
    score_scale = HEAD_SIZE ** (-0.5)

    def block_scores(index):
        key_first = index * key_block
        key_part = lax.dynamic_slice_in_dim(key_by_head, key_first, key_block, 1)
        scores = (
            jnp.einsum("hrd,hkd->hrk", query_rows, key_part, preferred_element_type=jnp.float32)
            * score_scale
        )
        key_pos = key_first + jnp.arange(key_block, dtype=jnp.int32)
        key_seg = lax.dynamic_slice_in_dim(seg_all, key_first, key_block, 0)
        allowed = (key_pos[None, :] <= row_pos[:, None]) & (key_seg[None, :] == row_seg[:, None])
        return jnp.where(allowed[None], scores, -jnp.inf)

    def max_step(index, running):
        return jnp.maximum(running, jnp.max(block_scores(index), axis=-1))

    row_max = lax.fori_loop(0, block_count, max_step, sink_rows)

    def sum_step(index, carried):
        weighted, denom = carried
        probs = jnp.exp(block_scores(index) - row_max[..., None]).astype(jnp.bfloat16)
        value_part = lax.dynamic_slice_in_dim(value_by_head, index * key_block, key_block, 1)
        weighted = weighted + jnp.einsum(
            "hrk,hkd->hrd", probs, value_part, preferred_element_type=jnp.float32
        )
        denom = denom + jnp.sum(probs, axis=-1, dtype=jnp.float32)
        return (weighted, denom)

    init_pair = (
        jnp.zeros((kv_heads, row_total, HEAD_SIZE), jnp.float32),
        jnp.zeros((kv_heads, row_total), jnp.float32),
    )
    weighted, denom = lax.fori_loop(0, block_count, sum_step, init_pair)
    denom = denom + jnp.exp(sink_rows - row_max)
    mixed = (weighted / denom[..., None]).astype(jnp.bfloat16)
    mixed = (
        mixed.reshape(kv_heads, heads_per_group, tok_count, HEAD_SIZE)
        .transpose(2, 0, 1, 3)
        .reshape(tok_count, query_cols)
    )
    out_terms = (
        jnp.einsum(
            "tc,efc->tef", mixed[:, :out_split], out_weight_first, preferred_element_type=jnp.float32
        )
        + jnp.einsum(
            "tc,efc->tef", mixed[:, out_split:], out_weight_second, preferred_element_type=jnp.float32
        )
    ).reshape(tok_count, -1)
    model_width = out_terms.shape[1]
    out_pieces = out_terms.astype(jnp.bfloat16).reshape(tok_count, mp_devs, model_width // mp_devs)
    out_got = lax.all_to_all(
        out_pieces.transpose(1, 0, 2), "mp", split_axis=0, concat_axis=0, tiled=True
    )
    attn_part = jnp.sum(out_got.astype(jnp.float32), axis=0)
    first_out = (local_rows.astype(jnp.float32) + attn_part).astype(jnp.bfloat16)
    top_count = routes.shape[2]
    local_experts = expert_in.shape[0]
    expert_count = local_experts * expert_devs
    capacity = 3 * tok_count * top_count // (2 * expert_count)
    chosen = routes[0].reshape(tok_count * top_count)
    onehot = (chosen[:, None] == jnp.arange(expert_count, dtype=jnp.int32)[None, :]).astype(
        jnp.int32
    )
    ranks = jnp.sum((jnp.cumsum(onehot, axis=0) - onehot) * onehot, axis=1)
    target = chosen * capacity + ranks
    source_row = (
        jnp.full((expert_count * capacity,), tok_count, jnp.int32)
        .at[target]
        .set(jnp.arange(tok_count * top_count, dtype=jnp.int32) // top_count)
    )
    padded = jnp.concatenate(
        [first_out, jnp.zeros((1, first_out.shape[1]), jnp.bfloat16)], axis=0
    )
    outgoing = padded[source_row].reshape(expert_count, capacity, padded.shape[1])
    arrived = lax.all_to_all(outgoing, "expert", split_axis=0, concat_axis=0, tiled=True)
    arrived_rows = arrived.reshape(expert_count * capacity, arrived.shape[2])
    inputs = rms_norm(lax.all_gather(arrived_rows, "mp", axis=1, tiled=True), moe_gain)
    w_in = expert_in[0]
    gate_val = jnp.dot(inputs, w_in[0], preferred_element_type=jnp.float32)
    up_val = jnp.dot(inputs, w_in[1], preferred_element_type=jnp.float32)
    gate_val = jnp.minimum(gate_val, clamp_limit)
    up_val = jnp.clip(up_val, -clamp_limit, clamp_limit)
    activated = ((up_val + 1.0) * gate_val * jax.nn.sigmoid(glu_alpha * gate_val)).astype(
        jnp.bfloat16
    )
    partials = jnp.einsum(
        "rh,hjf->jrf",
        activated,
        expert_down[0].reshape(expert_down.shape[1], mp_devs, -1),
        preferred_element_type=jnp.float32,
    )
    expert_out = lax.psum_scatter(
        partials.astype(jnp.bfloat16), "mp", scatter_dimension=0, tiled=True
    ).reshape(expert_count, capacity, -1)
    local_width = expert_out.shape[2]
    returned = lax.all_to_all(expert_out, "expert", split_axis=0, concat_axis=0, tiled=True)
    picked = returned.reshape(expert_count * capacity, local_width)[target].reshape(
        tok_count, top_count, local_width
    )
    moe_sum = jnp.sum(picked.astype(jnp.float32) * route_weights[0][..., None], axis=1)
    hidden = (first_out.astype(jnp.float32) + moe_sum).astype(jnp.bfloat16)
    return (hidden[None], key_rotary[None], value_fresh[None])


def solution(mesh):
    placed = (
        P("batch", "expert", "mp"),
        P("batch", None),
        P(),
        P("expert", "mp"),
        P("expert", "mp"),
        P("expert", "mp"),
        P("mp", "expert"),
        P("mp"),
        P(),
        P("expert", None, None, "mp"),
        P("expert", "mp", None),
        P("batch", "expert", None),
        P("batch", "expert", None),
    )
    return jax.shard_map(
        shards,
        mesh=mesh,
        in_specs=placed,
        out_specs=(
            P("batch", "expert", "mp"),
            P("batch", "expert", "mp"),
            P("batch", "expert", "mp"),
        ),
        check_vma=False,
    )
```

```python
import math

import jax
import jax.numpy as jnp
from jax import lax
from jax.sharding import PartitionSpec as P

HEAD_SIZE = 64


eps = 1e-05
rope_base = 150000.0
clamp_limit = 7.0
glu_alpha = 1.702


def rms_norm(row_block, gain):
    values = row_block.astype(jnp.float32)
    inv_scale = lax.rsqrt(jnp.mean(values * values, axis=-1, keepdims=True) + eps)
    return (values * inv_scale * gain).astype(jnp.bfloat16)


def apply_rotary(values, token_positions):
    half_dim = values.shape[-1] // 2
    inv_freq = jnp.power(
        rope_base, -2.0 * jnp.arange(half_dim, dtype=jnp.float32) / values.shape[-1]
    )
    rot_angle = token_positions.astype(jnp.float32)[:, None] * inv_freq[None, :]
    cosine = jnp.cos(rot_angle)[:, None, :]
    sine_val = jnp.sin(rot_angle)[:, None, :]
    first_half = values[..., :half_dim]
    second_half = values[..., half_dim:]
    return jnp.concatenate(
        [
            first_half * cosine - second_half * sine_val,
            second_half * cosine + first_half * sine_val,
        ],
        axis=-1,
    )


def gather_by_exchange(block, axis_name):
    count = lax.axis_size(axis_name)
    spread = jnp.broadcast_to(block[None], (count,) + block.shape)
    got = lax.all_to_all(spread, axis_name, split_axis=0, concat_axis=0, tiled=True)
    return got.reshape((count * block.shape[0],) + block.shape[1:])


def expert_rows(row_block, w_in, w_down):
    gate_val = jnp.dot(row_block, w_in[0], preferred_element_type=jnp.float32)
    up_val = jnp.dot(row_block, w_in[1], preferred_element_type=jnp.float32)
    gate_val = jnp.minimum(gate_val, clamp_limit)
    up_val = jnp.clip(up_val, -clamp_limit, clamp_limit)
    activated = ((up_val + 1.0) * gate_val * jax.nn.sigmoid(glu_alpha * gate_val)).astype(
        jnp.bfloat16
    )
    return jnp.dot(activated, w_down, preferred_element_type=jnp.float32)


def shards(
    tokens,
    segments,
    attn_gain,
    w_query,
    key_weight,
    value_weight,
    w_out,
    sink_head_logit,
    moe_gain,
    expert_in,
    expert_down,
    routes,
    route_weights,
):
    local_rows = tokens[0]
    tok_count = local_rows.shape[0]
    expert_devs = lax.axis_size("expert")
    row_start = lax.axis_index("expert") * tok_count
    mp_devs = lax.axis_size("mp")
    whole_rows = (
        gather_by_exchange(local_rows.T, "mp").reshape(-1, tok_count).T
    )
    input_normalised = rms_norm(whole_rows, attn_gain)
    query_cols = w_query.shape[1]
    kv_cols = key_weight.shape[1]
    big_weights = lax.all_gather(jnp.concatenate([w_query, w_out.T], axis=1), "expert", axis=0)
    query_weight = big_weights[:, :, :query_cols]
    out_weight_t = big_weights[:, :, query_cols:]
    kv_weight = gather_by_exchange(jnp.concatenate([key_weight, value_weight], axis=1), "expert")
    query_raw = jnp.einsum(
        "tef,efc->tc",
        input_normalised.reshape(tok_count, expert_devs, -1),
        query_weight,
        preferred_element_type=jnp.float32,
    )
    kv_raw = jnp.dot(input_normalised, kv_weight, preferred_element_type=jnp.float32)
    key_raw = kv_raw[:, :kv_cols]
    value_raw = kv_raw[:, kv_cols:]
    token_positions = row_start + jnp.arange(tok_count, dtype=jnp.int32)
    query_by_head = query_cols // HEAD_SIZE
    kv_heads = kv_cols // HEAD_SIZE
    heads_per_group = query_by_head // kv_heads
    query_matrix = apply_rotary(
        query_raw.reshape(tok_count, query_by_head, HEAD_SIZE), token_positions
    ).astype(jnp.bfloat16)
    key_rotary = (
        apply_rotary(key_raw.reshape(tok_count, kv_heads, HEAD_SIZE), token_positions)
        .astype(jnp.bfloat16)
        .reshape(tok_count, kv_cols)
    )
    value_fresh = value_raw.astype(jnp.bfloat16)
    kv_all = gather_by_exchange(jnp.concatenate([key_rotary, value_fresh], axis=1), "expert")
    keys_all = kv_all[:, :kv_cols]
    values_all = kv_all[:, kv_cols:]
    seq_len = keys_all.shape[0]
    seg_all = segments[0]
    seg_local = lax.dynamic_slice_in_dim(seg_all, row_start, tok_count)
    row_total = heads_per_group * tok_count
    query_rows = (
        query_matrix.reshape(tok_count, kv_heads, heads_per_group, HEAD_SIZE)
        .transpose(1, 2, 0, 3)
        .reshape(kv_heads, row_total, HEAD_SIZE)
    )
    key_by_head = keys_all.reshape(seq_len, kv_heads, HEAD_SIZE).transpose(1, 0, 2)
    value_by_head = values_all.reshape(seq_len, kv_heads, HEAD_SIZE).transpose(1, 0, 2)
    row_pos = jnp.tile(token_positions, heads_per_group)
    row_seg = jnp.tile(seg_local, heads_per_group)
    sink_rows = jnp.repeat(sink_head_logit.reshape(kv_heads, heads_per_group), tok_count, axis=1)
    key_block = math.gcd(seq_len, 512)
    block_count = seq_len // key_block
    score_scale = HEAD_SIZE ** (-0.5)

    def block_scores(index):
        key_first = index * key_block
        key_part = lax.dynamic_slice_in_dim(key_by_head, key_first, key_block, 1)
        scores = (
            jnp.einsum("hrd,hkd->hrk", query_rows, key_part, preferred_element_type=jnp.float32)
            * score_scale
        )
        key_pos = key_first + jnp.arange(key_block, dtype=jnp.int32)
        key_seg = lax.dynamic_slice_in_dim(seg_all, key_first, key_block, 0)
        allowed = (key_pos[None, :] <= row_pos[:, None]) & (key_seg[None, :] == row_seg[:, None])
        return jnp.where(allowed[None], scores, -jnp.inf)

    def max_step(index, running):
        return jnp.maximum(running, jnp.max(block_scores(index), axis=-1))

    row_max = lax.fori_loop(0, block_count, max_step, sink_rows)

    def sum_step(index, carried):
        weighted, denom = carried
        probs = jnp.exp(block_scores(index) - row_max[..., None]).astype(jnp.bfloat16)
        value_part = lax.dynamic_slice_in_dim(value_by_head, index * key_block, key_block, 1)
        weighted = weighted + jnp.einsum(
            "hrk,hkd->hrd", probs, value_part, preferred_element_type=jnp.float32
        )
        denom = denom + jnp.sum(probs, axis=-1, dtype=jnp.float32)
        return (weighted, denom)

    init_pair = (
        jnp.zeros((kv_heads, row_total, HEAD_SIZE), jnp.float32),
        jnp.zeros((kv_heads, row_total), jnp.float32),
    )
    weighted, denom = lax.fori_loop(0, block_count, sum_step, init_pair)
    denom = denom + jnp.exp(sink_rows - row_max)
    mixed = (weighted / denom[..., None]).astype(jnp.bfloat16)
    mixed = (
        mixed.reshape(kv_heads, heads_per_group, tok_count, HEAD_SIZE)
        .transpose(2, 0, 1, 3)
        .reshape(tok_count, query_cols)
    )
    out_terms_t = jnp.einsum(
        "efc,tc->eft", out_weight_t, mixed, preferred_element_type=jnp.float32
    )
    model_width = out_terms_t.shape[0] * out_terms_t.shape[1]
    out_pieces = out_terms_t.astype(jnp.bfloat16).reshape(mp_devs, model_width // mp_devs, tok_count)
    out_got = lax.all_to_all(out_pieces, "mp", split_axis=0, concat_axis=0, tiled=True)
    attn_part = jnp.sum(out_got.astype(jnp.float32), axis=0).T
    first_out = (local_rows.astype(jnp.float32) + attn_part).astype(jnp.bfloat16)
    top_count = routes.shape[2]
    local_experts = expert_in.shape[0]
    expert_count = local_experts * expert_devs
    capacity = 3 * tok_count * top_count // (2 * expert_count)
    chosen = routes[0].reshape(tok_count * top_count)
    onehot = (chosen[:, None] == jnp.arange(expert_count, dtype=jnp.int32)[None, :]).astype(
        jnp.int32
    )
    ranks = jnp.sum((jnp.cumsum(onehot, axis=0) - onehot) * onehot, axis=1)
    target = chosen * capacity + ranks
    source_row = (
        jnp.full((expert_count * capacity,), tok_count, jnp.int32)
        .at[target]
        .set(jnp.arange(tok_count * top_count, dtype=jnp.int32) // top_count)
    )
    padded = jnp.concatenate(
        [first_out, jnp.zeros((1, first_out.shape[1]), jnp.bfloat16)], axis=0
    )
    outgoing = padded[source_row].reshape(expert_count, capacity, padded.shape[1])
    arrived = lax.all_to_all(outgoing, "expert", split_axis=0, concat_axis=0, tiled=True)
    arrived_rows = arrived.reshape(expert_count * capacity, arrived.shape[2])
    inputs = rms_norm(lax.all_gather(arrived_rows, "mp", axis=1, tiled=True), moe_gain)
    w_in = expert_in[0]
    gate_val = jnp.dot(inputs, w_in[0], preferred_element_type=jnp.float32)
    up_val = jnp.dot(inputs, w_in[1], preferred_element_type=jnp.float32)
    gate_val = jnp.minimum(gate_val, clamp_limit)
    up_val = jnp.clip(up_val, -clamp_limit, clamp_limit)
    activated = ((up_val + 1.0) * gate_val * jax.nn.sigmoid(glu_alpha * gate_val)).astype(
        jnp.bfloat16
    )
    activated = lax.optimization_barrier(activated)
    partials = jnp.einsum(
        "rh,hjf->jrf",
        activated,
        expert_down[0].reshape(expert_down.shape[1], mp_devs, -1),
        preferred_element_type=jnp.float32,
    )
    expert_out = lax.psum_scatter(
        partials.astype(jnp.bfloat16), "mp", scatter_dimension=0, tiled=True
    ).reshape(expert_count, capacity, -1)
    local_width = expert_out.shape[2]
    returned = lax.all_to_all(expert_out, "expert", split_axis=0, concat_axis=0, tiled=True)
    picked = returned.reshape(expert_count * capacity, local_width)[target].reshape(
        tok_count, top_count, local_width
    )
    moe_sum = jnp.sum(picked.astype(jnp.float32) * route_weights[0][..., None], axis=1)
    hidden = (first_out.astype(jnp.float32) + moe_sum).astype(jnp.bfloat16)
    return (hidden[None], key_rotary[None], value_fresh[None])


def solution(mesh):
    placed = (
        P("batch", "expert", "mp"),
        P("batch", None),
        P(),
        P("expert", "mp"),
        P("expert", "mp"),
        P("expert", "mp"),
        P("mp", "expert"),
        P("mp"),
        P(),
        P("expert", None, None, "mp"),
        P("expert", "mp", None),
        P("batch", "expert", None),
        P("batch", "expert", None),
    )
    return jax.shard_map(
        shards,
        mesh=mesh,
        in_specs=placed,
        out_specs=(
            P("batch", "expert", "mp"),
            P("batch", "expert", "mp"),
            P("batch", "expert", "mp"),
        ),
        check_vma=False,
    )
```

```python
import math

import jax
import jax.numpy as jnp
from jax import lax
from jax.sharding import PartitionSpec as P

HEAD_SIZE = 64


eps = 1e-05
rope_base = 150000.0
clamp_limit = 7.0
glu_alpha = 1.702


def rms_norm(row_block, gain):
    values = row_block.astype(jnp.float32)
    inv_scale = lax.rsqrt(jnp.mean(values * values, axis=-1, keepdims=True) + eps)
    return (values * inv_scale * gain).astype(jnp.bfloat16)


def apply_rotary(values, token_positions):
    half_dim = values.shape[-1] // 2
    inv_freq = jnp.power(
        rope_base, -2.0 * jnp.arange(half_dim, dtype=jnp.float32) / values.shape[-1]
    )
    rot_angle = token_positions.astype(jnp.float32)[:, None] * inv_freq[None, :]
    cosine = jnp.cos(rot_angle)[:, None, :]
    sine_val = jnp.sin(rot_angle)[:, None, :]
    first_half = values[..., :half_dim]
    second_half = values[..., half_dim:]
    return jnp.concatenate(
        [
            first_half * cosine - second_half * sine_val,
            second_half * cosine + first_half * sine_val,
        ],
        axis=-1,
    )


def gather_by_exchange(block, axis_name):
    count = lax.axis_size(axis_name)
    spread = jnp.broadcast_to(block[None], (count,) + block.shape)
    got = lax.all_to_all(spread, axis_name, split_axis=0, concat_axis=0, tiled=True)
    return got.reshape((count * block.shape[0],) + block.shape[1:])


def expert_rows(row_block, w_in, w_down):
    gate_val = jnp.dot(row_block, w_in[0], preferred_element_type=jnp.float32)
    up_val = jnp.dot(row_block, w_in[1], preferred_element_type=jnp.float32)
    gate_val = jnp.minimum(gate_val, clamp_limit)
    up_val = jnp.clip(up_val, -clamp_limit, clamp_limit)
    activated = ((up_val + 1.0) * gate_val * jax.nn.sigmoid(glu_alpha * gate_val)).astype(
        jnp.bfloat16
    )
    return jnp.dot(activated, w_down, preferred_element_type=jnp.float32)


def shards(
    tokens,
    segments,
    attn_gain,
    w_query,
    key_weight,
    value_weight,
    w_out,
    sink_head_logit,
    moe_gain,
    expert_in,
    expert_down,
    routes,
    route_weights,
):
    local_rows = tokens[0]
    tok_count = local_rows.shape[0]
    expert_devs = lax.axis_size("expert")
    row_start = lax.axis_index("expert") * tok_count
    mp_devs = lax.axis_size("mp")
    whole_rows = (
        gather_by_exchange(local_rows.T, "mp").reshape(-1, tok_count).T
    )
    input_normalised = rms_norm(whole_rows, attn_gain)
    query_cols = w_query.shape[1]
    kv_cols = key_weight.shape[1]
    shard_rows = w_query.shape[0]
    padded_rows = -(-shard_rows // 8) * 8
    big_weights = lax.all_gather(
        jnp.pad(
            jnp.concatenate([w_query, w_out.T], axis=1), ((0, padded_rows - shard_rows), (0, 0))
        ),
        "expert",
        axis=0,
    )
    query_weight = big_weights[:, :, :query_cols].reshape(expert_devs * padded_rows, query_cols)
    out_weight_t = big_weights[:, :, query_cols:]
    kv_weight = gather_by_exchange(jnp.concatenate([key_weight, value_weight], axis=1), "expert")
    normed_padded = jnp.pad(
        input_normalised.reshape(tok_count, expert_devs, shard_rows),
        ((0, 0), (0, 0), (0, padded_rows - shard_rows)),
    ).reshape(tok_count, expert_devs * padded_rows)
    query_raw = jnp.dot(normed_padded, query_weight, preferred_element_type=jnp.float32)
    kv_raw = jnp.dot(input_normalised, kv_weight, preferred_element_type=jnp.float32)
    key_raw = kv_raw[:, :kv_cols]
    value_raw = kv_raw[:, kv_cols:]
    token_positions = row_start + jnp.arange(tok_count, dtype=jnp.int32)
    query_by_head = query_cols // HEAD_SIZE
    kv_heads = kv_cols // HEAD_SIZE
    heads_per_group = query_by_head // kv_heads
    query_matrix = apply_rotary(
        query_raw.reshape(tok_count, query_by_head, HEAD_SIZE), token_positions
    ).astype(jnp.bfloat16)
    key_rotary = (
        apply_rotary(key_raw.reshape(tok_count, kv_heads, HEAD_SIZE), token_positions)
        .astype(jnp.bfloat16)
        .reshape(tok_count, kv_cols)
    )
    value_fresh = value_raw.astype(jnp.bfloat16)
    kv_all = gather_by_exchange(jnp.concatenate([key_rotary, value_fresh], axis=1), "expert")
    keys_all = kv_all[:, :kv_cols]
    values_all = kv_all[:, kv_cols:]
    seq_len = keys_all.shape[0]
    seg_all = segments[0]
    seg_local = lax.dynamic_slice_in_dim(seg_all, row_start, tok_count)
    row_total = heads_per_group * tok_count
    query_rows = (
        query_matrix.reshape(tok_count, kv_heads, heads_per_group, HEAD_SIZE)
        .transpose(1, 2, 0, 3)
        .reshape(kv_heads, row_total, HEAD_SIZE)
    )
    key_by_head = keys_all.reshape(seq_len, kv_heads, HEAD_SIZE).transpose(1, 0, 2)
    value_by_head = values_all.reshape(seq_len, kv_heads, HEAD_SIZE).transpose(1, 0, 2)
    row_pos = jnp.tile(token_positions, heads_per_group)
    row_seg = jnp.tile(seg_local, heads_per_group)
    sink_rows = jnp.repeat(sink_head_logit.reshape(kv_heads, heads_per_group), tok_count, axis=1)
    key_block = math.gcd(seq_len, 512)
    block_count = seq_len // key_block
    score_scale = HEAD_SIZE ** (-0.5)

    def block_scores(index):
        key_first = index * key_block
        key_part = lax.dynamic_slice_in_dim(key_by_head, key_first, key_block, 1)
        scores = (
            jnp.einsum("hrd,hkd->hrk", query_rows, key_part, preferred_element_type=jnp.float32)
            * score_scale
        )
        key_pos = key_first + jnp.arange(key_block, dtype=jnp.int32)
        key_seg = lax.dynamic_slice_in_dim(seg_all, key_first, key_block, 0)
        allowed = (key_pos[None, :] <= row_pos[:, None]) & (key_seg[None, :] == row_seg[:, None])
        return jnp.where(allowed[None], scores, -jnp.inf)

    def max_step(index, running):
        return jnp.maximum(running, jnp.max(block_scores(index), axis=-1))

    row_max = lax.fori_loop(0, block_count, max_step, sink_rows)

    def sum_step(index, carried):
        weighted, denom = carried
        probs = jnp.exp(block_scores(index) - row_max[..., None]).astype(jnp.bfloat16)
        value_part = lax.dynamic_slice_in_dim(value_by_head, index * key_block, key_block, 1)
        weighted = weighted + jnp.einsum(
            "hrk,hkd->hrd", probs, value_part, preferred_element_type=jnp.float32
        )
        denom = denom + jnp.sum(probs, axis=-1, dtype=jnp.float32)
        return (weighted, denom)

    init_pair = (
        jnp.zeros((kv_heads, row_total, HEAD_SIZE), jnp.float32),
        jnp.zeros((kv_heads, row_total), jnp.float32),
    )
    weighted, denom = lax.fori_loop(0, block_count, sum_step, init_pair)
    denom = denom + jnp.exp(sink_rows - row_max)
    mixed = (weighted / denom[..., None]).astype(jnp.bfloat16)
    mixed = (
        mixed.reshape(kv_heads, heads_per_group, tok_count, HEAD_SIZE)
        .transpose(2, 0, 1, 3)
        .reshape(tok_count, query_cols)
    )
    out_terms_t = jnp.einsum(
        "efc,tc->eft", out_weight_t, mixed, preferred_element_type=jnp.float32
    )[:, :shard_rows]
    model_width = out_terms_t.shape[0] * out_terms_t.shape[1]
    out_pieces = out_terms_t.astype(jnp.bfloat16).reshape(mp_devs, model_width // mp_devs, tok_count)
    out_got = lax.all_to_all(out_pieces, "mp", split_axis=0, concat_axis=0, tiled=True)
    attn_part = jnp.sum(out_got.astype(jnp.float32), axis=0).T
    first_out = (local_rows.astype(jnp.float32) + attn_part).astype(jnp.bfloat16)
    top_count = routes.shape[2]
    local_experts = expert_in.shape[0]
    expert_count = local_experts * expert_devs
    capacity = 3 * tok_count * top_count // (2 * expert_count)
    chosen = routes[0].reshape(tok_count * top_count)
    onehot = (chosen[:, None] == jnp.arange(expert_count, dtype=jnp.int32)[None, :]).astype(
        jnp.int32
    )
    ranks = jnp.sum((jnp.cumsum(onehot, axis=0) - onehot) * onehot, axis=1)
    target = chosen * capacity + ranks
    source_row = (
        jnp.full((expert_count * capacity,), tok_count, jnp.int32)
        .at[target]
        .set(jnp.arange(tok_count * top_count, dtype=jnp.int32) // top_count)
    )
    padded = jnp.concatenate(
        [first_out, jnp.zeros((1, first_out.shape[1]), jnp.bfloat16)], axis=0
    )
    outgoing = padded[source_row].reshape(expert_count, capacity, padded.shape[1])
    arrived = lax.all_to_all(outgoing, "expert", split_axis=0, concat_axis=0, tiled=True)
    arrived_rows = arrived.reshape(expert_count * capacity, arrived.shape[2])
    inputs = rms_norm(lax.all_gather(arrived_rows, "mp", axis=1, tiled=True), moe_gain)
    w_in = expert_in[0]
    gate_val = jnp.dot(inputs, w_in[0], preferred_element_type=jnp.float32)
    up_val = jnp.dot(inputs, w_in[1], preferred_element_type=jnp.float32)
    gate_val = jnp.minimum(gate_val, clamp_limit)
    up_val = jnp.clip(up_val, -clamp_limit, clamp_limit)
    activated = ((up_val + 1.0) * gate_val * jax.nn.sigmoid(glu_alpha * gate_val)).astype(
        jnp.bfloat16
    )
    activated = lax.optimization_barrier(activated)
    partials = jnp.einsum(
        "rh,hjf->jrf",
        activated,
        expert_down[0].reshape(expert_down.shape[1], mp_devs, -1),
        preferred_element_type=jnp.float32,
    )
    expert_out = lax.psum_scatter(
        partials.astype(jnp.bfloat16), "mp", scatter_dimension=0, tiled=True
    ).reshape(expert_count, capacity, -1)
    local_width = expert_out.shape[2]
    returned = lax.all_to_all(expert_out, "expert", split_axis=0, concat_axis=0, tiled=True)
    picked = returned.reshape(expert_count * capacity, local_width)[target].reshape(
        tok_count, top_count, local_width
    )
    moe_sum = jnp.sum(picked.astype(jnp.float32) * route_weights[0][..., None], axis=1)
    hidden = (first_out.astype(jnp.float32) + moe_sum).astype(jnp.bfloat16)
    return (hidden[None], key_rotary[None], value_fresh[None])


def solution(mesh):
    placed = (
        P("batch", "expert", "mp"),
        P("batch", None),
        P(),
        P("expert", "mp"),
        P("expert", "mp"),
        P("expert", "mp"),
        P("mp", "expert"),
        P("mp"),
        P(),
        P("expert", None, None, "mp"),
        P("expert", "mp", None),
        P("batch", "expert", None),
        P("batch", "expert", None),
    )
    return jax.shard_map(
        shards,
        mesh=mesh,
        in_specs=placed,
        out_specs=(
            P("batch", "expert", "mp"),
            P("batch", "expert", "mp"),
            P("batch", "expert", "mp"),
        ),
        check_vma=False,
    )
```

```python
import math

import jax
import jax.numpy as jnp
from jax import lax
from jax.sharding import PartitionSpec as P

HEAD_SIZE = 64


eps = 1e-05
rope_base = 150000.0
clamp_limit = 7.0
glu_alpha = 1.702


def rms_norm(row_block, gain):
    values = row_block.astype(jnp.float32)
    inv_scale = lax.rsqrt(jnp.mean(values * values, axis=-1, keepdims=True) + eps)
    return (values * inv_scale * gain).astype(jnp.bfloat16)


def apply_rotary(values, token_positions):
    half_dim = values.shape[-1] // 2
    inv_freq = jnp.power(
        rope_base, -2.0 * jnp.arange(half_dim, dtype=jnp.float32) / values.shape[-1]
    )
    rot_angle = token_positions.astype(jnp.float32)[:, None] * inv_freq[None, :]
    cosine = jnp.cos(rot_angle)[:, None, :]
    sine_val = jnp.sin(rot_angle)[:, None, :]
    first_half = values[..., :half_dim]
    second_half = values[..., half_dim:]
    return jnp.concatenate(
        [
            first_half * cosine - second_half * sine_val,
            second_half * cosine + first_half * sine_val,
        ],
        axis=-1,
    )


def gather_by_exchange(block, axis_name):
    count = lax.axis_size(axis_name)
    spread = jnp.broadcast_to(block[None], (count,) + block.shape)
    got = lax.all_to_all(spread, axis_name, split_axis=0, concat_axis=0, tiled=True)
    return got.reshape((count * block.shape[0],) + block.shape[1:])


def expert_rows(row_block, w_in, w_down):
    gate_val = jnp.dot(row_block, w_in[0], preferred_element_type=jnp.float32)
    up_val = jnp.dot(row_block, w_in[1], preferred_element_type=jnp.float32)
    gate_val = jnp.minimum(gate_val, clamp_limit)
    up_val = jnp.clip(up_val, -clamp_limit, clamp_limit)
    activated = ((up_val + 1.0) * gate_val * jax.nn.sigmoid(glu_alpha * gate_val)).astype(
        jnp.bfloat16
    )
    return jnp.dot(activated, w_down, preferred_element_type=jnp.float32)


def shards(
    tokens,
    segments,
    attn_gain,
    w_query,
    key_weight,
    value_weight,
    w_out,
    sink_head_logit,
    moe_gain,
    expert_in,
    expert_down,
    routes,
    route_weights,
):
    local_rows = tokens[0]
    tok_count = local_rows.shape[0]
    expert_devs = lax.axis_size("expert")
    row_start = lax.axis_index("expert") * tok_count
    mp_devs = lax.axis_size("mp")
    whole_rows = (
        gather_by_exchange(local_rows.T, "mp").reshape(-1, tok_count).T
    )
    input_normalised = rms_norm(whole_rows, attn_gain)
    query_cols = w_query.shape[1]
    kv_cols = key_weight.shape[1]
    big_weights = lax.all_gather(jnp.concatenate([w_query, w_out.T], axis=1), "expert", axis=0)
    query_weight = big_weights[:, :, :query_cols]
    out_weight_t = big_weights[:, :, query_cols:]
    kv_weight = gather_by_exchange(jnp.concatenate([key_weight, value_weight], axis=1), "expert")
    query_raw = jnp.einsum(
        "tef,efc->tc",
        input_normalised.reshape(tok_count, expert_devs, -1),
        query_weight,
        preferred_element_type=jnp.float32,
    )
    kv_raw = jnp.dot(input_normalised, kv_weight, preferred_element_type=jnp.float32)
    key_raw = kv_raw[:, :kv_cols]
    value_raw = kv_raw[:, kv_cols:]
    token_positions = row_start + jnp.arange(tok_count, dtype=jnp.int32)
    query_by_head = query_cols // HEAD_SIZE
    kv_heads = kv_cols // HEAD_SIZE
    heads_per_group = query_by_head // kv_heads
    query_matrix = apply_rotary(
        query_raw.reshape(tok_count, query_by_head, HEAD_SIZE), token_positions
    ).astype(jnp.bfloat16)
    key_rotary = (
        apply_rotary(key_raw.reshape(tok_count, kv_heads, HEAD_SIZE), token_positions)
        .astype(jnp.bfloat16)
        .reshape(tok_count, kv_cols)
    )
    value_fresh = value_raw.astype(jnp.bfloat16)
    kv_all = gather_by_exchange(jnp.concatenate([key_rotary, value_fresh], axis=1), "expert")
    keys_all = kv_all[:, :kv_cols]
    values_all = kv_all[:, kv_cols:]
    seq_len = keys_all.shape[0]
    seg_all = segments[0]
    seg_local = lax.dynamic_slice_in_dim(seg_all, row_start, tok_count)
    row_total = heads_per_group * tok_count
    query_rows = (
        query_matrix.reshape(tok_count, kv_heads, heads_per_group, HEAD_SIZE)
        .transpose(1, 2, 0, 3)
        .reshape(kv_heads, row_total, HEAD_SIZE)
    )
    key_by_head = keys_all.reshape(seq_len, kv_heads, HEAD_SIZE).transpose(1, 0, 2)
    value_by_head = values_all.reshape(seq_len, kv_heads, HEAD_SIZE).transpose(1, 0, 2)
    row_pos = jnp.tile(token_positions, heads_per_group)
    row_seg = jnp.tile(seg_local, heads_per_group)
    sink_rows = jnp.repeat(sink_head_logit.reshape(kv_heads, heads_per_group), tok_count, axis=1)
    key_block = math.gcd(seq_len, 1024)
    block_count = seq_len // key_block
    score_scale = HEAD_SIZE ** (-0.5)

    def block_scores(index):
        key_first = index * key_block
        key_part = lax.dynamic_slice_in_dim(key_by_head, key_first, key_block, 1)
        scores = (
            jnp.einsum("hrd,hkd->hrk", query_rows, key_part, preferred_element_type=jnp.float32)
            * score_scale
        )
        key_pos = key_first + jnp.arange(key_block, dtype=jnp.int32)
        key_seg = lax.dynamic_slice_in_dim(seg_all, key_first, key_block, 0)
        allowed = (key_pos[None, :] <= row_pos[:, None]) & (key_seg[None, :] == row_seg[:, None])
        return jnp.where(allowed[None], scores, -jnp.inf)

    def max_step(index, running):
        return jnp.maximum(running, jnp.max(block_scores(index), axis=-1))

    row_max = lax.fori_loop(0, block_count, max_step, sink_rows)

    def sum_step(index, carried):
        weighted, denom = carried
        probs = jnp.exp(block_scores(index) - row_max[..., None]).astype(jnp.bfloat16)
        value_part = lax.dynamic_slice_in_dim(value_by_head, index * key_block, key_block, 1)
        weighted = weighted + jnp.einsum(
            "hrk,hkd->hrd", probs, value_part, preferred_element_type=jnp.float32
        )
        denom = denom + jnp.sum(probs, axis=-1, dtype=jnp.float32)
        return (weighted, denom)

    init_pair = (
        jnp.zeros((kv_heads, row_total, HEAD_SIZE), jnp.float32),
        jnp.zeros((kv_heads, row_total), jnp.float32),
    )
    weighted, denom = lax.fori_loop(0, block_count, sum_step, init_pair)
    denom = denom + jnp.exp(sink_rows - row_max)
    mixed = (weighted / denom[..., None]).astype(jnp.bfloat16)
    mixed = (
        mixed.reshape(kv_heads, heads_per_group, tok_count, HEAD_SIZE)
        .transpose(2, 0, 1, 3)
        .reshape(tok_count, query_cols)
    )
    out_terms_t = jnp.einsum(
        "efc,tc->eft", out_weight_t, mixed, preferred_element_type=jnp.float32
    )
    model_width = out_terms_t.shape[0] * out_terms_t.shape[1]
    out_pieces = out_terms_t.astype(jnp.bfloat16).reshape(mp_devs, model_width // mp_devs, tok_count)
    out_got = lax.all_to_all(out_pieces, "mp", split_axis=0, concat_axis=0, tiled=True)
    attn_part = jnp.sum(out_got.astype(jnp.float32), axis=0).T
    first_out = (local_rows.astype(jnp.float32) + attn_part).astype(jnp.bfloat16)
    top_count = routes.shape[2]
    local_experts = expert_in.shape[0]
    expert_count = local_experts * expert_devs
    capacity = 3 * tok_count * top_count // (2 * expert_count)
    chosen = routes[0].reshape(tok_count * top_count)
    onehot = (chosen[:, None] == jnp.arange(expert_count, dtype=jnp.int32)[None, :]).astype(
        jnp.int32
    )
    ranks = jnp.sum((jnp.cumsum(onehot, axis=0) - onehot) * onehot, axis=1)
    target = chosen * capacity + ranks
    source_row = (
        jnp.full((expert_count * capacity,), tok_count, jnp.int32)
        .at[target]
        .set(jnp.arange(tok_count * top_count, dtype=jnp.int32) // top_count)
    )
    padded = jnp.concatenate(
        [first_out, jnp.zeros((1, first_out.shape[1]), jnp.bfloat16)], axis=0
    )
    pick = (source_row[:, None] == jnp.arange(tok_count + 1, dtype=jnp.int32)[None, :]).astype(
        jnp.bfloat16
    )
    outgoing = (
        jnp.dot(pick, padded, preferred_element_type=jnp.float32)
        .astype(jnp.bfloat16)
        .reshape(expert_count, capacity, padded.shape[1])
    )
    arrived = lax.all_to_all(outgoing, "expert", split_axis=0, concat_axis=0, tiled=True)
    arrived_rows = arrived.reshape(expert_count * capacity, arrived.shape[2])
    inputs = rms_norm(lax.all_gather(arrived_rows, "mp", axis=1, tiled=True), moe_gain)
    w_in = expert_in[0]
    gate_val = jnp.dot(inputs, w_in[0], preferred_element_type=jnp.float32)
    up_val = jnp.dot(inputs, w_in[1], preferred_element_type=jnp.float32)
    gate_val = jnp.minimum(gate_val, clamp_limit)
    up_val = jnp.clip(up_val, -clamp_limit, clamp_limit)
    activated = ((up_val + 1.0) * gate_val * jax.nn.sigmoid(glu_alpha * gate_val)).astype(
        jnp.bfloat16
    )
    activated = lax.optimization_barrier(activated)
    partials = jnp.einsum(
        "rh,hjf->jrf",
        activated,
        expert_down[0].reshape(expert_down.shape[1], mp_devs, -1),
        preferred_element_type=jnp.float32,
    )
    expert_out = lax.psum_scatter(
        partials.astype(jnp.bfloat16), "mp", scatter_dimension=0, tiled=True
    ).reshape(expert_count, capacity, -1)
    local_width = expert_out.shape[2]
    returned = lax.all_to_all(expert_out, "expert", split_axis=0, concat_axis=0, tiled=True)
    picked = returned.reshape(expert_count * capacity, local_width)[target].reshape(
        tok_count, top_count, local_width
    )
    moe_sum = jnp.sum(picked.astype(jnp.float32) * route_weights[0][..., None], axis=1)
    hidden = (first_out.astype(jnp.float32) + moe_sum).astype(jnp.bfloat16)
    return (hidden[None], key_rotary[None], value_fresh[None])


def solution(mesh):
    placed = (
        P("batch", "expert", "mp"),
        P("batch", None),
        P(),
        P("expert", "mp"),
        P("expert", "mp"),
        P("expert", "mp"),
        P("mp", "expert"),
        P("mp"),
        P(),
        P("expert", None, None, "mp"),
        P("expert", "mp", None),
        P("batch", "expert", None),
        P("batch", "expert", None),
    )
    return jax.shard_map(
        shards,
        mesh=mesh,
        in_specs=placed,
        out_specs=(
            P("batch", "expert", "mp"),
            P("batch", "expert", "mp"),
            P("batch", "expert", "mp"),
        ),
        check_vma=False,
    )
```

```python
import math

import jax
import jax.numpy as jnp
from jax import lax
from jax.sharding import PartitionSpec as P

HEAD_SIZE = 64


eps = 1e-05
rope_base = 150000.0
clamp_limit = 7.0
glu_alpha = 1.702


def rms_norm(row_block, gain):
    values = row_block.astype(jnp.float32)
    inv_scale = lax.rsqrt(jnp.mean(values * values, axis=-1, keepdims=True) + eps)
    return (values * inv_scale * gain).astype(jnp.bfloat16)


def apply_rotary(values, token_positions):
    half_dim = values.shape[-1] // 2
    inv_freq = jnp.power(
        rope_base, -2.0 * jnp.arange(half_dim, dtype=jnp.float32) / values.shape[-1]
    )
    rot_angle = token_positions.astype(jnp.float32)[:, None] * inv_freq[None, :]
    cosine = jnp.cos(rot_angle)[:, None, :]
    sine_val = jnp.sin(rot_angle)[:, None, :]
    first_half = values[..., :half_dim]
    second_half = values[..., half_dim:]
    return jnp.concatenate(
        [
            first_half * cosine - second_half * sine_val,
            second_half * cosine + first_half * sine_val,
        ],
        axis=-1,
    )


def gather_by_exchange(block, axis_name):
    count = lax.axis_size(axis_name)
    spread = jnp.broadcast_to(block[None], (count,) + block.shape)
    got = lax.all_to_all(spread, axis_name, split_axis=0, concat_axis=0, tiled=True)
    return got.reshape((count * block.shape[0],) + block.shape[1:])


def expert_rows(row_block, w_in, w_down):
    gate_val = jnp.dot(row_block, w_in[0], preferred_element_type=jnp.float32)
    up_val = jnp.dot(row_block, w_in[1], preferred_element_type=jnp.float32)
    gate_val = jnp.minimum(gate_val, clamp_limit)
    up_val = jnp.clip(up_val, -clamp_limit, clamp_limit)
    activated = ((up_val + 1.0) * gate_val * jax.nn.sigmoid(glu_alpha * gate_val)).astype(
        jnp.bfloat16
    )
    return jnp.dot(activated, w_down, preferred_element_type=jnp.float32)


def shards(
    tokens,
    segments,
    attn_gain,
    w_query,
    key_weight,
    value_weight,
    w_out,
    sink_head_logit,
    moe_gain,
    expert_in,
    expert_down,
    routes,
    route_weights,
):
    local_rows = tokens[0]
    tok_count = local_rows.shape[0]
    expert_devs = lax.axis_size("expert")
    row_start = lax.axis_index("expert") * tok_count
    mp_devs = lax.axis_size("mp")
    whole_rows = (
        gather_by_exchange(local_rows.T, "mp").reshape(-1, tok_count).T
    )
    input_normalised = rms_norm(whole_rows, attn_gain)
    query_cols = w_query.shape[1]
    kv_cols = key_weight.shape[1]
    big_weights = lax.all_gather(jnp.concatenate([w_query, w_out.T], axis=1), "expert", axis=0)
    query_weight = big_weights[:, :, :query_cols]
    out_weight_t = big_weights[:, :, query_cols:]
    kv_weight = gather_by_exchange(jnp.concatenate([key_weight, value_weight], axis=1), "expert")
    query_raw = jnp.einsum(
        "tef,efc->tc",
        input_normalised.reshape(tok_count, expert_devs, -1),
        query_weight,
        preferred_element_type=jnp.float32,
    )
    kv_raw = jnp.dot(input_normalised, kv_weight, preferred_element_type=jnp.float32)
    key_raw = kv_raw[:, :kv_cols]
    value_raw = kv_raw[:, kv_cols:]
    token_positions = row_start + jnp.arange(tok_count, dtype=jnp.int32)
    query_by_head = query_cols // HEAD_SIZE
    kv_heads = kv_cols // HEAD_SIZE
    heads_per_group = query_by_head // kv_heads
    query_matrix = apply_rotary(
        query_raw.reshape(tok_count, query_by_head, HEAD_SIZE), token_positions
    ).astype(jnp.bfloat16)
    key_rotary = (
        apply_rotary(key_raw.reshape(tok_count, kv_heads, HEAD_SIZE), token_positions)
        .astype(jnp.bfloat16)
        .reshape(tok_count, kv_cols)
    )
    value_fresh = value_raw.astype(jnp.bfloat16)
    kv_all = gather_by_exchange(jnp.concatenate([key_rotary, value_fresh], axis=1), "expert")
    keys_all = kv_all[:, :kv_cols]
    values_all = kv_all[:, kv_cols:]
    seq_len = keys_all.shape[0]
    seg_all = segments[0]
    seg_local = lax.dynamic_slice_in_dim(seg_all, row_start, tok_count)
    row_total = heads_per_group * tok_count
    query_rows = (
        query_matrix.reshape(tok_count, kv_heads, heads_per_group, HEAD_SIZE)
        .transpose(1, 2, 0, 3)
        .reshape(kv_heads, row_total, HEAD_SIZE)
    )
    key_by_head = keys_all.reshape(seq_len, kv_heads, HEAD_SIZE).transpose(1, 0, 2)
    value_by_head = values_all.reshape(seq_len, kv_heads, HEAD_SIZE).transpose(1, 0, 2)
    row_pos = jnp.tile(token_positions, heads_per_group)
    row_seg = jnp.tile(seg_local, heads_per_group)
    sink_rows = jnp.repeat(sink_head_logit.reshape(kv_heads, heads_per_group), tok_count, axis=1)
    key_block = math.gcd(seq_len, 2048)
    block_count = seq_len // key_block
    score_scale = HEAD_SIZE ** (-0.5)

    def block_scores(index):
        key_first = index * key_block
        key_part = lax.dynamic_slice_in_dim(key_by_head, key_first, key_block, 1)
        scores = (
            jnp.einsum("hrd,hkd->hrk", query_rows, key_part, preferred_element_type=jnp.float32)
            * score_scale
        )
        key_pos = key_first + jnp.arange(key_block, dtype=jnp.int32)
        key_seg = lax.dynamic_slice_in_dim(seg_all, key_first, key_block, 0)
        allowed = (key_pos[None, :] <= row_pos[:, None]) & (key_seg[None, :] == row_seg[:, None])
        return jnp.where(allowed[None], scores, -jnp.inf)

    def max_step(index, running):
        return jnp.maximum(running, jnp.max(block_scores(index), axis=-1))

    row_max = lax.fori_loop(0, block_count, max_step, sink_rows)

    def sum_step(index, carried):
        weighted, denom = carried
        probs = jnp.exp(block_scores(index) - row_max[..., None]).astype(jnp.bfloat16)
        value_part = lax.dynamic_slice_in_dim(value_by_head, index * key_block, key_block, 1)
        weighted = weighted + jnp.einsum(
            "hrk,hkd->hrd", probs, value_part, preferred_element_type=jnp.float32
        )
        denom = denom + jnp.sum(probs, axis=-1, dtype=jnp.float32)
        return (weighted, denom)

    init_pair = (
        jnp.zeros((kv_heads, row_total, HEAD_SIZE), jnp.float32),
        jnp.zeros((kv_heads, row_total), jnp.float32),
    )
    weighted, denom = lax.fori_loop(0, block_count, sum_step, init_pair)
    denom = denom + jnp.exp(sink_rows - row_max)
    mixed = (weighted / denom[..., None]).astype(jnp.bfloat16)
    mixed = (
        mixed.reshape(kv_heads, heads_per_group, tok_count, HEAD_SIZE)
        .transpose(2, 0, 1, 3)
        .reshape(tok_count, query_cols)
    )
    out_terms_t = jnp.einsum(
        "efc,tc->eft", out_weight_t, mixed, preferred_element_type=jnp.float32
    )
    model_width = out_terms_t.shape[0] * out_terms_t.shape[1]
    out_pieces = out_terms_t.astype(jnp.bfloat16).reshape(mp_devs, model_width // mp_devs, tok_count)
    out_got = lax.all_to_all(out_pieces, "mp", split_axis=0, concat_axis=0, tiled=True)
    attn_part = jnp.sum(out_got.astype(jnp.float32), axis=0).T
    first_out = (local_rows.astype(jnp.float32) + attn_part).astype(jnp.bfloat16)
    top_count = routes.shape[2]
    local_experts = expert_in.shape[0]
    expert_count = local_experts * expert_devs
    capacity = 3 * tok_count * top_count // (2 * expert_count)
    chosen = routes[0].reshape(tok_count * top_count)
    onehot = (chosen[:, None] == jnp.arange(expert_count, dtype=jnp.int32)[None, :]).astype(
        jnp.int32
    )
    ranks = jnp.sum((jnp.cumsum(onehot, axis=0) - onehot) * onehot, axis=1)
    target = chosen * capacity + ranks
    source_row = (
        jnp.full((expert_count * capacity,), tok_count, jnp.int32)
        .at[target]
        .set(jnp.arange(tok_count * top_count, dtype=jnp.int32) // top_count)
    )
    padded = jnp.concatenate(
        [first_out, jnp.zeros((1, first_out.shape[1]), jnp.bfloat16)], axis=0
    )
    pick = (source_row[:, None] == jnp.arange(tok_count + 1, dtype=jnp.int32)[None, :]).astype(
        jnp.bfloat16
    )
    outgoing = (
        jnp.dot(pick, padded, preferred_element_type=jnp.float32)
        .astype(jnp.bfloat16)
        .reshape(expert_count, capacity, padded.shape[1])
    )
    arrived = lax.all_to_all(outgoing, "expert", split_axis=0, concat_axis=0, tiled=True)
    arrived_rows = arrived.reshape(expert_count * capacity, arrived.shape[2])
    inputs = rms_norm(lax.all_gather(arrived_rows, "mp", axis=1, tiled=True), moe_gain)
    w_in = expert_in[0]
    gate_val = jnp.dot(inputs, w_in[0], preferred_element_type=jnp.float32)
    up_val = jnp.dot(inputs, w_in[1], preferred_element_type=jnp.float32)
    gate_val = jnp.minimum(gate_val, clamp_limit)
    up_val = jnp.clip(up_val, -clamp_limit, clamp_limit)
    activated = ((up_val + 1.0) * gate_val * jax.nn.sigmoid(glu_alpha * gate_val)).astype(
        jnp.bfloat16
    )
    activated = lax.optimization_barrier(activated)
    partials = jnp.einsum(
        "rh,hjf->jrf",
        activated,
        expert_down[0].reshape(expert_down.shape[1], mp_devs, -1),
        preferred_element_type=jnp.float32,
    )
    expert_out = lax.psum_scatter(
        partials.astype(jnp.bfloat16), "mp", scatter_dimension=0, tiled=True
    ).reshape(expert_count, capacity, -1)
    local_width = expert_out.shape[2]
    returned = lax.all_to_all(expert_out, "expert", split_axis=0, concat_axis=0, tiled=True)
    slot_pick = (
        target[:, None] == jnp.arange(expert_count * capacity, dtype=jnp.int32)[None, :]
    ).astype(jnp.bfloat16)
    picked = jnp.dot(
        slot_pick,
        returned.reshape(expert_count * capacity, local_width),
        preferred_element_type=jnp.float32,
    ).reshape(tok_count, top_count, local_width)
    moe_sum = jnp.sum(picked.astype(jnp.float32) * route_weights[0][..., None], axis=1)
    hidden = (first_out.astype(jnp.float32) + moe_sum).astype(jnp.bfloat16)
    return (hidden[None], key_rotary[None], value_fresh[None])


def solution(mesh):
    placed = (
        P("batch", "expert", "mp"),
        P("batch", None),
        P(),
        P("expert", "mp"),
        P("expert", "mp"),
        P("expert", "mp"),
        P("mp", "expert"),
        P("mp"),
        P(),
        P("expert", None, None, "mp"),
        P("expert", "mp", None),
        P("batch", "expert", None),
        P("batch", "expert", None),
    )
    return jax.shard_map(
        shards,
        mesh=mesh,
        in_specs=placed,
        out_specs=(
            P("batch", "expert", "mp"),
            P("batch", "expert", "mp"),
            P("batch", "expert", "mp"),
        ),
        check_vma=False,
    )
```

```python
import math

import jax
import jax.numpy as jnp
from jax import lax
from jax.sharding import PartitionSpec as P

HEAD_SIZE = 64


eps = 1e-05
rope_base = 150000.0
clamp_limit = 7.0
glu_alpha = 1.702


def rms_norm(row_block, gain):
    values = row_block.astype(jnp.float32)
    inv_scale = lax.rsqrt(jnp.mean(values * values, axis=-1, keepdims=True) + eps)
    return (values * inv_scale * gain).astype(jnp.bfloat16)


def apply_rotary(values, token_positions):
    half_dim = values.shape[-1] // 2
    inv_freq = jnp.power(
        rope_base, -2.0 * jnp.arange(half_dim, dtype=jnp.float32) / values.shape[-1]
    )
    rot_angle = token_positions.astype(jnp.float32)[:, None] * inv_freq[None, :]
    cosine = jnp.cos(rot_angle)[:, None, :]
    sine_val = jnp.sin(rot_angle)[:, None, :]
    first_half = values[..., :half_dim]
    second_half = values[..., half_dim:]
    return jnp.concatenate(
        [
            first_half * cosine - second_half * sine_val,
            second_half * cosine + first_half * sine_val,
        ],
        axis=-1,
    )


def gather_by_exchange(block, axis_name):
    count = lax.axis_size(axis_name)
    spread = jnp.broadcast_to(block[None], (count,) + block.shape)
    got = lax.all_to_all(spread, axis_name, split_axis=0, concat_axis=0, tiled=True)
    return got.reshape((count * block.shape[0],) + block.shape[1:])


def expert_rows(row_block, w_in, w_down):
    gate_val = jnp.dot(row_block, w_in[0], preferred_element_type=jnp.float32)
    up_val = jnp.dot(row_block, w_in[1], preferred_element_type=jnp.float32)
    gate_val = jnp.minimum(gate_val, clamp_limit)
    up_val = jnp.clip(up_val, -clamp_limit, clamp_limit)
    activated = ((up_val + 1.0) * gate_val * jax.nn.sigmoid(glu_alpha * gate_val)).astype(
        jnp.bfloat16
    )
    return jnp.dot(activated, w_down, preferred_element_type=jnp.float32)


def shards(
    tokens,
    segments,
    attn_gain,
    w_query,
    key_weight,
    value_weight,
    w_out,
    sink_head_logit,
    moe_gain,
    expert_in,
    expert_down,
    routes,
    route_weights,
):
    local_rows = tokens[0]
    tok_count = local_rows.shape[0]
    expert_devs = lax.axis_size("expert")
    row_start = lax.axis_index("expert") * tok_count
    mp_devs = lax.axis_size("mp")
    whole_rows = (
        gather_by_exchange(local_rows.T, "mp").reshape(-1, tok_count).T
    )
    input_normalised = rms_norm(whole_rows, attn_gain)
    query_cols = w_query.shape[1]
    kv_cols = key_weight.shape[1]
    shard_rows = w_query.shape[0]
    padded_rows = -(-shard_rows // 8) * 8
    big_weights = lax.all_gather(
        jnp.pad(
            jnp.concatenate([w_query, w_out.T], axis=1), ((0, padded_rows - shard_rows), (0, 0))
        ),
        "expert",
        axis=0,
    )
    query_weight = big_weights[:, :, :query_cols].reshape(expert_devs * padded_rows, query_cols)
    out_weight_t = big_weights[:, :, query_cols:]
    kv_weight = gather_by_exchange(jnp.concatenate([key_weight, value_weight], axis=1), "expert")
    normed_padded = jnp.pad(
        input_normalised.reshape(tok_count, expert_devs, shard_rows),
        ((0, 0), (0, 0), (0, padded_rows - shard_rows)),
    ).reshape(tok_count, expert_devs * padded_rows)
    query_raw = jnp.dot(normed_padded, query_weight, preferred_element_type=jnp.float32)
    kv_raw = jnp.dot(input_normalised, kv_weight, preferred_element_type=jnp.float32)
    key_raw = kv_raw[:, :kv_cols]
    value_raw = kv_raw[:, kv_cols:]
    token_positions = row_start + jnp.arange(tok_count, dtype=jnp.int32)
    query_by_head = query_cols // HEAD_SIZE
    kv_heads = kv_cols // HEAD_SIZE
    heads_per_group = query_by_head // kv_heads
    query_matrix = apply_rotary(
        query_raw.reshape(tok_count, query_by_head, HEAD_SIZE), token_positions
    ).astype(jnp.bfloat16)
    key_rotary = (
        apply_rotary(key_raw.reshape(tok_count, kv_heads, HEAD_SIZE), token_positions)
        .astype(jnp.bfloat16)
        .reshape(tok_count, kv_cols)
    )
    value_fresh = value_raw.astype(jnp.bfloat16)
    kv_all = gather_by_exchange(jnp.concatenate([key_rotary, value_fresh], axis=1), "expert")
    keys_all = kv_all[:, :kv_cols]
    values_all = kv_all[:, kv_cols:]
    seq_len = keys_all.shape[0]
    seg_all = segments[0]
    seg_local = lax.dynamic_slice_in_dim(seg_all, row_start, tok_count)
    row_total = heads_per_group * tok_count
    query_rows = (
        query_matrix.reshape(tok_count, kv_heads, heads_per_group, HEAD_SIZE)
        .transpose(1, 2, 0, 3)
        .reshape(kv_heads, row_total, HEAD_SIZE)
    )
    key_by_head = keys_all.reshape(seq_len, kv_heads, HEAD_SIZE).transpose(1, 0, 2)
    value_by_head = values_all.reshape(seq_len, kv_heads, HEAD_SIZE).transpose(1, 0, 2)
    row_pos = jnp.tile(token_positions, heads_per_group)
    row_seg = jnp.tile(seg_local, heads_per_group)
    sink_rows = jnp.repeat(sink_head_logit.reshape(kv_heads, heads_per_group), tok_count, axis=1)
    key_block = math.gcd(seq_len, 2048)
    block_count = seq_len // key_block
    score_scale = HEAD_SIZE ** (-0.5)

    def block_scores(index):
        key_first = index * key_block
        key_part = lax.dynamic_slice_in_dim(key_by_head, key_first, key_block, 1)
        scores = (
            jnp.einsum("hrd,hkd->hrk", query_rows, key_part, preferred_element_type=jnp.float32)
            * score_scale
        )
        key_pos = key_first + jnp.arange(key_block, dtype=jnp.int32)
        key_seg = lax.dynamic_slice_in_dim(seg_all, key_first, key_block, 0)
        allowed = (key_pos[None, :] <= row_pos[:, None]) & (key_seg[None, :] == row_seg[:, None])
        return jnp.where(allowed[None], scores, -jnp.inf)

    def max_step(index, running):
        return jnp.maximum(running, jnp.max(block_scores(index), axis=-1))

    row_max = lax.fori_loop(0, block_count, max_step, sink_rows)

    def sum_step(index, carried):
        weighted, denom = carried
        probs = jnp.exp(block_scores(index) - row_max[..., None]).astype(jnp.bfloat16)
        value_part = lax.dynamic_slice_in_dim(value_by_head, index * key_block, key_block, 1)
        weighted = weighted + jnp.einsum(
            "hrk,hkd->hrd", probs, value_part, preferred_element_type=jnp.float32
        )
        denom = denom + jnp.sum(probs, axis=-1, dtype=jnp.float32)
        return (weighted, denom)

    init_pair = (
        jnp.zeros((kv_heads, row_total, HEAD_SIZE), jnp.float32),
        jnp.zeros((kv_heads, row_total), jnp.float32),
    )
    weighted, denom = lax.fori_loop(0, block_count, sum_step, init_pair)
    denom = denom + jnp.exp(sink_rows - row_max)
    mixed = (weighted / denom[..., None]).astype(jnp.bfloat16)
    mixed = (
        mixed.reshape(kv_heads, heads_per_group, tok_count, HEAD_SIZE)
        .transpose(2, 0, 1, 3)
        .reshape(tok_count, query_cols)
    )
    out_terms_t = jnp.einsum(
        "efc,tc->eft", out_weight_t, mixed, preferred_element_type=jnp.float32
    )[:, :shard_rows]
    model_width = out_terms_t.shape[0] * out_terms_t.shape[1]
    out_pieces = out_terms_t.astype(jnp.bfloat16).reshape(mp_devs, model_width // mp_devs, tok_count)
    out_got = lax.all_to_all(out_pieces, "mp", split_axis=0, concat_axis=0, tiled=True)
    attn_part = jnp.sum(out_got.astype(jnp.float32), axis=0).T
    first_out = (local_rows.astype(jnp.float32) + attn_part).astype(jnp.bfloat16)
    top_count = routes.shape[2]
    local_experts = expert_in.shape[0]
    expert_count = local_experts * expert_devs
    capacity = 3 * tok_count * top_count // (2 * expert_count)
    chosen = routes[0].reshape(tok_count * top_count)
    onehot = (chosen[:, None] == jnp.arange(expert_count, dtype=jnp.int32)[None, :]).astype(
        jnp.int32
    )
    ranks = jnp.sum((jnp.cumsum(onehot, axis=0) - onehot) * onehot, axis=1)
    target = chosen * capacity + ranks
    source_row = (
        jnp.full((expert_count * capacity,), tok_count, jnp.int32)
        .at[target]
        .set(jnp.arange(tok_count * top_count, dtype=jnp.int32) // top_count)
    )
    padded = jnp.concatenate(
        [first_out, jnp.zeros((1, first_out.shape[1]), jnp.bfloat16)], axis=0
    )
    pick = (source_row[:, None] == jnp.arange(tok_count + 1, dtype=jnp.int32)[None, :]).astype(
        jnp.bfloat16
    )
    outgoing = (
        jnp.dot(pick, padded, preferred_element_type=jnp.float32)
        .astype(jnp.bfloat16)
        .reshape(expert_count, capacity, padded.shape[1])
    )
    arrived = lax.all_to_all(outgoing, "expert", split_axis=0, concat_axis=0, tiled=True)
    arrived_rows = arrived.reshape(expert_count * capacity, arrived.shape[2])
    inputs = rms_norm(lax.all_gather(arrived_rows, "mp", axis=1, tiled=True), moe_gain)
    w_in = expert_in[0]
    gate_val = jnp.dot(inputs, w_in[0], preferred_element_type=jnp.float32)
    up_val = jnp.dot(inputs, w_in[1], preferred_element_type=jnp.float32)
    gate_val = jnp.minimum(gate_val, clamp_limit)
    up_val = jnp.clip(up_val, -clamp_limit, clamp_limit)
    activated = ((up_val + 1.0) * gate_val * jax.nn.sigmoid(glu_alpha * gate_val)).astype(
        jnp.bfloat16
    )
    activated = lax.optimization_barrier(activated)
    partials = jnp.einsum(
        "rh,hjf->jrf",
        activated,
        expert_down[0].reshape(expert_down.shape[1], mp_devs, -1),
        preferred_element_type=jnp.float32,
    )
    expert_out = lax.psum_scatter(
        partials.astype(jnp.bfloat16), "mp", scatter_dimension=0, tiled=True
    ).reshape(expert_count, capacity, -1)
    local_width = expert_out.shape[2]
    returned = lax.all_to_all(expert_out, "expert", split_axis=0, concat_axis=0, tiled=True)
    slot_pick = (
        target[:, None] == jnp.arange(expert_count * capacity, dtype=jnp.int32)[None, :]
    ).astype(jnp.bfloat16)
    picked = jnp.dot(
        slot_pick,
        returned.reshape(expert_count * capacity, local_width),
        preferred_element_type=jnp.float32,
    ).reshape(tok_count, top_count, local_width)
    moe_sum = jnp.sum(picked.astype(jnp.float32) * route_weights[0][..., None], axis=1)
    hidden = (first_out.astype(jnp.float32) + moe_sum).astype(jnp.bfloat16)
    return (hidden[None], key_rotary[None], value_fresh[None])


def solution(mesh):
    placed = (
        P("batch", "expert", "mp"),
        P("batch", None),
        P(),
        P("expert", "mp"),
        P("expert", "mp"),
        P("expert", "mp"),
        P("mp", "expert"),
        P("mp"),
        P(),
        P("expert", None, None, "mp"),
        P("expert", "mp", None),
        P("batch", "expert", None),
        P("batch", "expert", None),
    )
    return jax.shard_map(
        shards,
        mesh=mesh,
        in_specs=placed,
        out_specs=(
            P("batch", "expert", "mp"),
            P("batch", "expert", "mp"),
            P("batch", "expert", "mp"),
        ),
        check_vma=False,
    )
```

```python
import math

import jax
import jax.numpy as jnp
from jax import lax
from jax.sharding import PartitionSpec as P

HEAD_SIZE = 64


eps = 1e-05
rope_base = 150000.0
clamp_limit = 7.0
glu_alpha = 1.702


def rms_norm(row_block, gain):
    values = row_block.astype(jnp.float32)
    inv_scale = lax.rsqrt(jnp.mean(values * values, axis=-1, keepdims=True) + eps)
    return (values * inv_scale * gain).astype(jnp.bfloat16)


def apply_rotary(values, token_positions):
    half_dim = values.shape[-1] // 2
    inv_freq = jnp.power(
        rope_base, -2.0 * jnp.arange(half_dim, dtype=jnp.float32) / values.shape[-1]
    )
    rot_angle = token_positions.astype(jnp.float32)[:, None] * inv_freq[None, :]
    cosine = jnp.cos(rot_angle)[:, None, :]
    sine_val = jnp.sin(rot_angle)[:, None, :]
    first_half = values[..., :half_dim]
    second_half = values[..., half_dim:]
    return jnp.concatenate(
        [
            first_half * cosine - second_half * sine_val,
            second_half * cosine + first_half * sine_val,
        ],
        axis=-1,
    )


def gather_by_exchange(block, axis_name):
    count = lax.axis_size(axis_name)
    spread = jnp.broadcast_to(block[None], (count,) + block.shape)
    got = lax.all_to_all(spread, axis_name, split_axis=0, concat_axis=0, tiled=True)
    return got.reshape((count * block.shape[0],) + block.shape[1:])


def expert_rows(row_block, w_in, w_down):
    gate_val = jnp.dot(row_block, w_in[0], preferred_element_type=jnp.float32)
    up_val = jnp.dot(row_block, w_in[1], preferred_element_type=jnp.float32)
    gate_val = jnp.minimum(gate_val, clamp_limit)
    up_val = jnp.clip(up_val, -clamp_limit, clamp_limit)
    activated = ((up_val + 1.0) * gate_val * jax.nn.sigmoid(glu_alpha * gate_val)).astype(
        jnp.bfloat16
    )
    return jnp.dot(activated, w_down, preferred_element_type=jnp.float32)


def shards(
    tokens,
    segments,
    attn_gain,
    w_query,
    key_weight,
    value_weight,
    w_out,
    sink_head_logit,
    moe_gain,
    expert_in,
    expert_down,
    routes,
    route_weights,
):
    local_rows = tokens[0]
    tok_count = local_rows.shape[0]
    expert_devs = lax.axis_size("expert")
    row_start = lax.axis_index("expert") * tok_count
    mp_devs = lax.axis_size("mp")
    whole_rows = (
        gather_by_exchange(local_rows.T, "mp").reshape(-1, tok_count).T
    )
    input_normalised = rms_norm(whole_rows, attn_gain)
    query_cols = w_query.shape[1]
    kv_cols = key_weight.shape[1]
    shard_rows = w_query.shape[0]
    padded_rows = -(-shard_rows // 8) * 8
    big_weights = lax.all_gather(
        jnp.pad(
            jnp.concatenate([w_query, w_out.T], axis=1), ((0, padded_rows - shard_rows), (0, 0))
        ),
        "expert",
        axis=0,
    )
    query_weight = big_weights[:, :, :query_cols].reshape(expert_devs * padded_rows, query_cols)
    out_weight_t = big_weights[:, :, query_cols:]
    kv_weight = gather_by_exchange(jnp.concatenate([key_weight, value_weight], axis=1), "expert")
    normed_padded = jnp.pad(
        input_normalised.reshape(tok_count, expert_devs, shard_rows),
        ((0, 0), (0, 0), (0, padded_rows - shard_rows)),
    ).reshape(tok_count, expert_devs * padded_rows)
    query_raw = jnp.dot(normed_padded, query_weight, preferred_element_type=jnp.float32)
    kv_raw = jnp.dot(input_normalised, kv_weight, preferred_element_type=jnp.float32)
    key_raw = kv_raw[:, :kv_cols]
    value_raw = kv_raw[:, kv_cols:]
    token_positions = row_start + jnp.arange(tok_count, dtype=jnp.int32)
    query_by_head = query_cols // HEAD_SIZE
    kv_heads = kv_cols // HEAD_SIZE
    heads_per_group = query_by_head // kv_heads
    query_matrix = apply_rotary(
        query_raw.reshape(tok_count, query_by_head, HEAD_SIZE), token_positions
    ).astype(jnp.bfloat16)
    key_rotary = (
        apply_rotary(key_raw.reshape(tok_count, kv_heads, HEAD_SIZE), token_positions)
        .astype(jnp.bfloat16)
        .reshape(tok_count, kv_cols)
    )
    value_fresh = value_raw.astype(jnp.bfloat16)
    kv_all = gather_by_exchange(jnp.concatenate([key_rotary, value_fresh], axis=1), "expert")
    keys_all = kv_all[:, :kv_cols]
    values_all = kv_all[:, kv_cols:]
    seq_len = keys_all.shape[0]
    seg_all = segments[0]
    seg_local = lax.dynamic_slice_in_dim(seg_all, row_start, tok_count)
    row_total = heads_per_group * tok_count
    query_rows = (
        query_matrix.reshape(tok_count, kv_heads, heads_per_group, HEAD_SIZE)
        .transpose(1, 2, 0, 3)
        .reshape(kv_heads, row_total, HEAD_SIZE)
    )
    key_by_head = keys_all.reshape(seq_len, kv_heads, HEAD_SIZE).transpose(1, 0, 2)
    value_by_head = values_all.reshape(seq_len, kv_heads, HEAD_SIZE).transpose(1, 0, 2)
    row_pos = jnp.tile(token_positions, heads_per_group)
    row_seg = jnp.tile(seg_local, heads_per_group)
    sink_rows = jnp.repeat(sink_head_logit.reshape(kv_heads, heads_per_group), tok_count, axis=1)
    key_block = math.gcd(seq_len, 2048)
    block_count = seq_len // key_block
    score_scale = HEAD_SIZE ** (-0.5)

    def block_scores(index):
        key_first = index * key_block
        key_part = lax.dynamic_slice_in_dim(key_by_head, key_first, key_block, 1)
        scores = (
            jnp.einsum("hrd,hkd->hrk", query_rows, key_part, preferred_element_type=jnp.float32)
            * score_scale
        )
        key_pos = key_first + jnp.arange(key_block, dtype=jnp.int32)
        key_seg = lax.dynamic_slice_in_dim(seg_all, key_first, key_block, 0)
        allowed = (key_pos[None, :] <= row_pos[:, None]) & (key_seg[None, :] == row_seg[:, None])
        return jnp.where(allowed[None], scores, -jnp.inf)

    def max_step(index, running):
        return jnp.maximum(running, jnp.max(block_scores(index), axis=-1))

    row_max = lax.fori_loop(0, block_count, max_step, sink_rows)

    def sum_step(index, carried):
        weighted, denom = carried
        probs = jnp.exp(block_scores(index) - row_max[..., None]).astype(jnp.bfloat16)
        value_part = lax.dynamic_slice_in_dim(value_by_head, index * key_block, key_block, 1)
        weighted = weighted + jnp.einsum(
            "hrk,hkd->hrd", probs, value_part, preferred_element_type=jnp.float32
        )
        denom = denom + jnp.sum(probs, axis=-1, dtype=jnp.float32)
        return (weighted, denom)

    init_pair = (
        jnp.zeros((kv_heads, row_total, HEAD_SIZE), jnp.float32),
        jnp.zeros((kv_heads, row_total), jnp.float32),
    )
    weighted, denom = lax.fori_loop(0, block_count, sum_step, init_pair)
    denom = denom + jnp.exp(sink_rows - row_max)
    mixed = (weighted / denom[..., None]).astype(jnp.bfloat16)
    mixed = (
        mixed.reshape(kv_heads, heads_per_group, tok_count, HEAD_SIZE)
        .transpose(2, 0, 1, 3)
        .reshape(tok_count, query_cols)
    )
    out_terms_t = jnp.einsum(
        "efc,tc->eft", out_weight_t, mixed, preferred_element_type=jnp.float32
    )[:, :shard_rows]
    model_width = out_terms_t.shape[0] * out_terms_t.shape[1]
    out_pieces = out_terms_t.astype(jnp.bfloat16).reshape(mp_devs, model_width // mp_devs, tok_count)
    out_got = lax.all_to_all(out_pieces, "mp", split_axis=0, concat_axis=0, tiled=True)
    attn_part = jnp.sum(out_got.astype(jnp.float32), axis=0).T
    first_out = (local_rows.astype(jnp.float32) + attn_part).astype(jnp.bfloat16)
    top_count = routes.shape[2]
    local_experts = expert_in.shape[0]
    expert_count = local_experts * expert_devs
    capacity = 3 * tok_count * top_count // (2 * expert_count)
    chosen = routes[0].reshape(tok_count * top_count)
    onehot = (chosen[:, None] == jnp.arange(expert_count, dtype=jnp.int32)[None, :]).astype(
        jnp.int32
    )
    ranks = jnp.sum((jnp.cumsum(onehot, axis=0) - onehot) * onehot, axis=1)
    target = chosen * capacity + ranks
    source_row = (
        jnp.full((expert_count * capacity,), tok_count, jnp.int32)
        .at[target]
        .set(jnp.arange(tok_count * top_count, dtype=jnp.int32) // top_count)
    )
    padded = jnp.concatenate(
        [first_out, jnp.zeros((1, first_out.shape[1]), jnp.bfloat16)], axis=0
    )
    pick = (source_row[:, None] == jnp.arange(tok_count + 1, dtype=jnp.int32)[None, :]).astype(
        jnp.bfloat16
    )
    outgoing = (
        jnp.dot(pick, padded, preferred_element_type=jnp.float32)
        .astype(jnp.bfloat16)
        .reshape(expert_count, capacity, padded.shape[1])
    )
    arrived = lax.all_to_all(outgoing, "expert", split_axis=0, concat_axis=0, tiled=True)
    arrived_rows = arrived.reshape(expert_count * capacity, arrived.shape[2])
    inputs = rms_norm(lax.all_gather(arrived_rows, "mp", axis=1, tiled=True), moe_gain)
    w_in = expert_in[0]
    hidden_cols = w_in.shape[2]
    inputs = lax.optimization_barrier(inputs)
    gate_up = jnp.dot(
        inputs, jnp.concatenate([w_in[0], w_in[1]], axis=1), preferred_element_type=jnp.float32
    )
    gate_val = gate_up[:, :hidden_cols]
    up_val = gate_up[:, hidden_cols:]
    gate_val = jnp.minimum(gate_val, clamp_limit)
    up_val = jnp.clip(up_val, -clamp_limit, clamp_limit)
    activated = ((up_val + 1.0) * gate_val * jax.nn.sigmoid(glu_alpha * gate_val)).astype(
        jnp.bfloat16
    )
    activated = lax.optimization_barrier(activated)
    partials = jnp.einsum(
        "rh,hjf->jrf",
        activated,
        expert_down[0].reshape(expert_down.shape[1], mp_devs, -1),
        preferred_element_type=jnp.float32,
    )
    expert_out = lax.psum_scatter(
        partials.astype(jnp.bfloat16), "mp", scatter_dimension=0, tiled=True
    ).reshape(expert_count, capacity, -1)
    local_width = expert_out.shape[2]
    returned = lax.all_to_all(expert_out, "expert", split_axis=0, concat_axis=0, tiled=True)
    slot_pick = (
        target[:, None] == jnp.arange(expert_count * capacity, dtype=jnp.int32)[None, :]
    ).astype(jnp.bfloat16)
    picked = jnp.dot(
        slot_pick,
        returned.reshape(expert_count * capacity, local_width),
        preferred_element_type=jnp.float32,
    ).reshape(tok_count, top_count, local_width)
    moe_sum = jnp.sum(picked.astype(jnp.float32) * route_weights[0][..., None], axis=1)
    hidden = (first_out.astype(jnp.float32) + moe_sum).astype(jnp.bfloat16)
    return (hidden[None], key_rotary[None], value_fresh[None])


def solution(mesh):
    placed = (
        P("batch", "expert", "mp"),
        P("batch", None),
        P(),
        P("expert", "mp"),
        P("expert", "mp"),
        P("expert", "mp"),
        P("mp", "expert"),
        P("mp"),
        P(),
        P("expert", None, None, "mp"),
        P("expert", "mp", None),
        P("batch", "expert", None),
        P("batch", "expert", None),
    )
    return jax.shard_map(
        shards,
        mesh=mesh,
        in_specs=placed,
        out_specs=(
            P("batch", "expert", "mp"),
            P("batch", "expert", "mp"),
            P("batch", "expert", "mp"),
        ),
        check_vma=False,
    )
```

```python
import math

import jax
import jax.numpy as jnp
from jax import lax
from jax.sharding import PartitionSpec as P

HEAD_SIZE = 64


eps = 1e-05
rope_base = 150000.0
clamp_limit = 7.0
glu_alpha = 1.702


def rms_norm(row_block, gain):
    values = row_block.astype(jnp.float32)
    inv_scale = lax.rsqrt(jnp.mean(values * values, axis=-1, keepdims=True) + eps)
    return (values * inv_scale * gain).astype(jnp.bfloat16)


def apply_rotary(values, token_positions):
    half_dim = values.shape[-1] // 2
    inv_freq = jnp.power(
        rope_base, -2.0 * jnp.arange(half_dim, dtype=jnp.float32) / values.shape[-1]
    )
    rot_angle = token_positions.astype(jnp.float32)[:, None] * inv_freq[None, :]
    cosine = jnp.cos(rot_angle)[:, None, :]
    sine_val = jnp.sin(rot_angle)[:, None, :]
    first_half = values[..., :half_dim]
    second_half = values[..., half_dim:]
    return jnp.concatenate(
        [
            first_half * cosine - second_half * sine_val,
            second_half * cosine + first_half * sine_val,
        ],
        axis=-1,
    )


def gather_by_exchange(block, axis_name):
    count = lax.axis_size(axis_name)
    spread = jnp.broadcast_to(block[None], (count,) + block.shape)
    got = lax.all_to_all(spread, axis_name, split_axis=0, concat_axis=0, tiled=True)
    return got.reshape((count * block.shape[0],) + block.shape[1:])


def expert_rows(row_block, w_in, w_down):
    gate_val = jnp.dot(row_block, w_in[0], preferred_element_type=jnp.float32)
    up_val = jnp.dot(row_block, w_in[1], preferred_element_type=jnp.float32)
    gate_val = jnp.minimum(gate_val, clamp_limit)
    up_val = jnp.clip(up_val, -clamp_limit, clamp_limit)
    activated = ((up_val + 1.0) * gate_val * jax.nn.sigmoid(glu_alpha * gate_val)).astype(
        jnp.bfloat16
    )
    return jnp.dot(activated, w_down, preferred_element_type=jnp.float32)


def shards(
    tokens,
    segments,
    attn_gain,
    w_query,
    key_weight,
    value_weight,
    w_out,
    sink_head_logit,
    moe_gain,
    expert_in,
    expert_down,
    routes,
    route_weights,
):
    local_rows = tokens[0]
    tok_count = local_rows.shape[0]
    expert_devs = lax.axis_size("expert")
    row_start = lax.axis_index("expert") * tok_count
    mp_devs = lax.axis_size("mp")
    whole_rows = (
        gather_by_exchange(local_rows.T, "mp").reshape(-1, tok_count).T
    )
    input_normalised = rms_norm(whole_rows, attn_gain)
    query_cols = w_query.shape[1]
    kv_cols = key_weight.shape[1]
    shard_rows = w_query.shape[0]
    padded_rows = -(-shard_rows // 8) * 8
    big_weights = lax.all_gather(
        jnp.pad(
            jnp.concatenate([w_query, w_out.T], axis=1), ((0, padded_rows - shard_rows), (0, 0))
        ),
        "expert",
        axis=0,
    )
    query_weight = big_weights[:, :, :query_cols].reshape(expert_devs * padded_rows, query_cols)
    out_weight_t = big_weights[:, :, query_cols:]
    kv_weight = gather_by_exchange(jnp.concatenate([key_weight, value_weight], axis=1), "expert")
    normed_padded = jnp.pad(
        input_normalised.reshape(tok_count, expert_devs, shard_rows),
        ((0, 0), (0, 0), (0, padded_rows - shard_rows)),
    ).reshape(tok_count, expert_devs * padded_rows)
    query_raw = jnp.dot(normed_padded, query_weight, preferred_element_type=jnp.float32)
    kv_raw = jnp.dot(input_normalised, kv_weight, preferred_element_type=jnp.float32)
    key_raw = kv_raw[:, :kv_cols]
    value_raw = kv_raw[:, kv_cols:]
    token_positions = row_start + jnp.arange(tok_count, dtype=jnp.int32)
    query_by_head = query_cols // HEAD_SIZE
    kv_heads = kv_cols // HEAD_SIZE
    heads_per_group = query_by_head // kv_heads
    query_matrix = apply_rotary(
        query_raw.reshape(tok_count, query_by_head, HEAD_SIZE), token_positions
    ).astype(jnp.bfloat16)
    key_rotary = (
        apply_rotary(key_raw.reshape(tok_count, kv_heads, HEAD_SIZE), token_positions)
        .astype(jnp.bfloat16)
        .reshape(tok_count, kv_cols)
    )
    value_fresh = value_raw.astype(jnp.bfloat16)
    kv_all = gather_by_exchange(jnp.concatenate([key_rotary, value_fresh], axis=1), "expert")
    keys_all = kv_all[:, :kv_cols]
    values_all = kv_all[:, kv_cols:]
    seq_len = keys_all.shape[0]
    seg_all = segments[0]
    seg_local = lax.dynamic_slice_in_dim(seg_all, row_start, tok_count)
    row_total = heads_per_group * tok_count
    query_rows = (
        query_matrix.reshape(tok_count, kv_heads, heads_per_group, HEAD_SIZE)
        .transpose(1, 2, 0, 3)
        .reshape(kv_heads, row_total, HEAD_SIZE)
    )
    key_by_head = keys_all.reshape(seq_len, kv_heads, HEAD_SIZE).transpose(1, 0, 2)
    value_by_head = values_all.reshape(seq_len, kv_heads, HEAD_SIZE).transpose(1, 0, 2)
    row_pos = jnp.tile(token_positions, heads_per_group)
    row_seg = jnp.tile(seg_local, heads_per_group)
    sink_rows = jnp.repeat(sink_head_logit.reshape(kv_heads, heads_per_group), tok_count, axis=1)
    key_block = math.gcd(seq_len, 2048)
    block_count = seq_len // key_block
    score_scale = HEAD_SIZE ** (-0.5)

    def block_scores(index):
        key_first = index * key_block
        key_part = lax.dynamic_slice_in_dim(key_by_head, key_first, key_block, 1)
        scores = (
            jnp.einsum("hrd,hkd->hrk", query_rows, key_part, preferred_element_type=jnp.float32)
            * score_scale
        )
        key_pos = key_first + jnp.arange(key_block, dtype=jnp.int32)
        key_seg = lax.dynamic_slice_in_dim(seg_all, key_first, key_block, 0)
        allowed = (key_pos[None, :] <= row_pos[:, None]) & (key_seg[None, :] == row_seg[:, None])
        return jnp.where(allowed[None], scores, -jnp.inf)

    def max_step(index, running):
        return jnp.maximum(running, jnp.max(block_scores(index), axis=-1))

    row_max = lax.fori_loop(0, block_count, max_step, sink_rows)

    def sum_step(index, carried):
        weighted, denom = carried
        probs = jnp.exp(block_scores(index) - row_max[..., None]).astype(jnp.bfloat16)
        value_part = lax.dynamic_slice_in_dim(value_by_head, index * key_block, key_block, 1)
        weighted = weighted + jnp.einsum(
            "hrk,hkd->hrd", probs, value_part, preferred_element_type=jnp.float32
        )
        denom = denom + jnp.sum(probs, axis=-1, dtype=jnp.float32)
        return (weighted, denom)

    init_pair = (
        jnp.zeros((kv_heads, row_total, HEAD_SIZE), jnp.float32),
        jnp.zeros((kv_heads, row_total), jnp.float32),
    )
    weighted, denom = lax.fori_loop(0, block_count, sum_step, init_pair)
    denom = denom + jnp.exp(sink_rows - row_max)
    mixed = (weighted / denom[..., None]).astype(jnp.bfloat16)
    mixed = (
        mixed.reshape(kv_heads, heads_per_group, tok_count, HEAD_SIZE)
        .transpose(2, 0, 1, 3)
        .reshape(tok_count, query_cols)
    )
    out_terms_t = jnp.einsum(
        "efc,tc->eft", out_weight_t, mixed, preferred_element_type=jnp.float32
    )[:, :shard_rows]
    model_width = out_terms_t.shape[0] * out_terms_t.shape[1]
    out_pieces = out_terms_t.astype(jnp.bfloat16).reshape(mp_devs, model_width // mp_devs, tok_count)
    out_got = lax.all_to_all(out_pieces, "mp", split_axis=0, concat_axis=0, tiled=True)
    attn_part = jnp.sum(out_got.astype(jnp.float32), axis=0).T
    first_out = (local_rows.astype(jnp.float32) + attn_part).astype(jnp.bfloat16)
    top_count = routes.shape[2]
    local_experts = expert_in.shape[0]
    expert_count = local_experts * expert_devs
    capacity = 3 * tok_count * top_count // (2 * expert_count)
    chosen = routes[0].reshape(tok_count * top_count)
    onehot = (chosen[:, None] == jnp.arange(expert_count, dtype=jnp.int32)[None, :]).astype(
        jnp.int32
    )
    ranks = jnp.sum((jnp.cumsum(onehot, axis=0) - onehot) * onehot, axis=1)
    target = chosen * capacity + ranks
    slot_of_route = (
        target[None, :] == jnp.arange(expert_count * capacity, dtype=jnp.int32)[:, None]
    ).astype(jnp.bfloat16)
    outgoing = (
        jnp.dot(
            slot_of_route,
            jnp.repeat(first_out, top_count, axis=0),
            preferred_element_type=jnp.float32,
        )
        .astype(jnp.bfloat16)
        .reshape(expert_count, capacity, first_out.shape[1])
    )
    arrived = lax.all_to_all(outgoing, "expert", split_axis=0, concat_axis=0, tiled=True)
    arrived_rows = arrived.reshape(expert_count * capacity, arrived.shape[2])
    inputs = rms_norm(lax.all_gather(arrived_rows, "mp", axis=1, tiled=True), moe_gain)
    w_in = expert_in[0]
    hidden_cols = w_in.shape[2]
    inputs = lax.optimization_barrier(inputs)
    gate_up = jnp.dot(
        inputs, jnp.concatenate([w_in[0], w_in[1]], axis=1), preferred_element_type=jnp.float32
    )
    gate_val = gate_up[:, :hidden_cols]
    up_val = gate_up[:, hidden_cols:]
    gate_val = jnp.minimum(gate_val, clamp_limit)
    up_val = jnp.clip(up_val, -clamp_limit, clamp_limit)
    activated = ((up_val + 1.0) * gate_val * jax.nn.sigmoid(glu_alpha * gate_val)).astype(
        jnp.bfloat16
    )
    activated = lax.optimization_barrier(activated)
    partials = jnp.einsum(
        "rh,hjf->jrf",
        activated,
        expert_down[0].reshape(expert_down.shape[1], mp_devs, -1),
        preferred_element_type=jnp.float32,
    )
    expert_out = lax.psum_scatter(
        partials.astype(jnp.bfloat16), "mp", scatter_dimension=0, tiled=True
    ).reshape(expert_count, capacity, -1)
    local_width = expert_out.shape[2]
    returned = lax.all_to_all(expert_out, "expert", split_axis=0, concat_axis=0, tiled=True)
    slot_pick = (
        target[:, None] == jnp.arange(expert_count * capacity, dtype=jnp.int32)[None, :]
    ).astype(jnp.bfloat16)
    picked = jnp.dot(
        slot_pick,
        returned.reshape(expert_count * capacity, local_width),
        preferred_element_type=jnp.float32,
    ).reshape(tok_count, top_count, local_width)
    moe_sum = jnp.sum(picked.astype(jnp.float32) * route_weights[0][..., None], axis=1)
    hidden = (first_out.astype(jnp.float32) + moe_sum).astype(jnp.bfloat16)
    return (hidden[None], key_rotary[None], value_fresh[None])


def solution(mesh):
    placed = (
        P("batch", "expert", "mp"),
        P("batch", None),
        P(),
        P("expert", "mp"),
        P("expert", "mp"),
        P("expert", "mp"),
        P("mp", "expert"),
        P("mp"),
        P(),
        P("expert", None, None, "mp"),
        P("expert", "mp", None),
        P("batch", "expert", None),
        P("batch", "expert", None),
    )
    return jax.shard_map(
        shards,
        mesh=mesh,
        in_specs=placed,
        out_specs=(
            P("batch", "expert", "mp"),
            P("batch", "expert", "mp"),
            P("batch", "expert", "mp"),
        ),
        check_vma=False,
    )
```

```python
import math

import jax
import jax.numpy as jnp
from jax import lax
from jax.sharding import PartitionSpec as P

HEAD_SIZE = 64


eps = 1e-05
rope_base = 150000.0
clamp_limit = 7.0
glu_alpha = 1.702


def rms_norm(row_block, gain):
    values = row_block.astype(jnp.float32)
    inv_scale = lax.rsqrt(jnp.mean(values * values, axis=-1, keepdims=True) + eps)
    return (values * inv_scale * gain).astype(jnp.bfloat16)


def apply_rotary(values, token_positions):
    half_dim = values.shape[-1] // 2
    inv_freq = jnp.power(
        rope_base, -2.0 * jnp.arange(half_dim, dtype=jnp.float32) / values.shape[-1]
    )
    rot_angle = token_positions.astype(jnp.float32)[:, None] * inv_freq[None, :]
    cosine = jnp.cos(rot_angle)[:, None, :]
    sine_val = jnp.sin(rot_angle)[:, None, :]
    first_half = values[..., :half_dim]
    second_half = values[..., half_dim:]
    return jnp.concatenate(
        [
            first_half * cosine - second_half * sine_val,
            second_half * cosine + first_half * sine_val,
        ],
        axis=-1,
    )


def gather_by_exchange(block, axis_name):
    count = lax.axis_size(axis_name)
    spread = jnp.broadcast_to(block[None], (count,) + block.shape)
    got = lax.all_to_all(spread, axis_name, split_axis=0, concat_axis=0, tiled=True)
    return got.reshape((count * block.shape[0],) + block.shape[1:])


def expert_rows(row_block, w_in, w_down):
    gate_val = jnp.dot(row_block, w_in[0], preferred_element_type=jnp.float32)
    up_val = jnp.dot(row_block, w_in[1], preferred_element_type=jnp.float32)
    gate_val = jnp.minimum(gate_val, clamp_limit)
    up_val = jnp.clip(up_val, -clamp_limit, clamp_limit)
    activated = ((up_val + 1.0) * gate_val * jax.nn.sigmoid(glu_alpha * gate_val)).astype(
        jnp.bfloat16
    )
    return jnp.dot(activated, w_down, preferred_element_type=jnp.float32)


def shards(
    tokens,
    segments,
    attn_gain,
    w_query,
    key_weight,
    value_weight,
    w_out,
    sink_head_logit,
    moe_gain,
    expert_in,
    expert_down,
    routes,
    route_weights,
):
    local_rows = tokens[0]
    tok_count = local_rows.shape[0]
    expert_devs = lax.axis_size("expert")
    row_start = lax.axis_index("expert") * tok_count
    mp_devs = lax.axis_size("mp")
    whole_rows = (
        gather_by_exchange(local_rows.T, "mp").reshape(-1, tok_count).T
    )
    input_normalised = rms_norm(whole_rows, attn_gain)
    query_cols = w_query.shape[1]
    kv_cols = key_weight.shape[1]
    shard_rows = w_query.shape[0]
    padded_rows = -(-shard_rows // 8) * 8
    big_weights = lax.all_gather(
        jnp.pad(
            jnp.concatenate([w_query, w_out.T], axis=1), ((0, padded_rows - shard_rows), (0, 0))
        ),
        "expert",
        axis=0,
    )
    query_weight = big_weights[:, :, :query_cols].reshape(expert_devs * padded_rows, query_cols)
    out_weight_t = big_weights[:, :, query_cols:]
    kv_weight = gather_by_exchange(jnp.concatenate([key_weight, value_weight], axis=1), "expert")
    normed_padded = jnp.pad(
        input_normalised.reshape(tok_count, expert_devs, shard_rows),
        ((0, 0), (0, 0), (0, padded_rows - shard_rows)),
    ).reshape(tok_count, expert_devs * padded_rows)
    query_raw = jnp.dot(normed_padded, query_weight, preferred_element_type=jnp.float32)
    kv_raw = jnp.dot(input_normalised, kv_weight, preferred_element_type=jnp.float32)
    key_raw = kv_raw[:, :kv_cols]
    value_raw = kv_raw[:, kv_cols:]
    token_positions = row_start + jnp.arange(tok_count, dtype=jnp.int32)
    query_by_head = query_cols // HEAD_SIZE
    kv_heads = kv_cols // HEAD_SIZE
    heads_per_group = query_by_head // kv_heads
    query_matrix = apply_rotary(
        query_raw.reshape(tok_count, query_by_head, HEAD_SIZE), token_positions
    ).astype(jnp.bfloat16)
    key_rotary = (
        apply_rotary(key_raw.reshape(tok_count, kv_heads, HEAD_SIZE), token_positions)
        .astype(jnp.bfloat16)
        .reshape(tok_count, kv_cols)
    )
    value_fresh = value_raw.astype(jnp.bfloat16)
    kv_all = gather_by_exchange(jnp.concatenate([key_rotary, value_fresh], axis=1), "expert")
    keys_all = kv_all[:, :kv_cols]
    values_all = kv_all[:, kv_cols:]
    seq_len = keys_all.shape[0]
    seg_all = segments[0]
    seg_local = lax.dynamic_slice_in_dim(seg_all, row_start, tok_count)
    row_total = heads_per_group * tok_count
    query_rows = (
        query_matrix.reshape(tok_count, kv_heads, heads_per_group, HEAD_SIZE)
        .transpose(1, 2, 0, 3)
        .reshape(kv_heads, row_total, HEAD_SIZE)
    )
    key_by_head = keys_all.reshape(seq_len, kv_heads, HEAD_SIZE).transpose(1, 0, 2)
    value_by_head = values_all.reshape(seq_len, kv_heads, HEAD_SIZE).transpose(1, 0, 2)
    row_pos = jnp.tile(token_positions, heads_per_group)
    row_seg = jnp.tile(seg_local, heads_per_group)
    sink_rows = jnp.repeat(sink_head_logit.reshape(kv_heads, heads_per_group), tok_count, axis=1)
    key_block = math.gcd(seq_len, 2048)
    block_count = seq_len // key_block
    score_scale = HEAD_SIZE ** (-0.5)

    def block_scores(index):
        key_first = index * key_block
        key_part = lax.dynamic_slice_in_dim(key_by_head, key_first, key_block, 1)
        scores = (
            jnp.einsum("hrd,hkd->hrk", query_rows, key_part, preferred_element_type=jnp.float32)
            * score_scale
        )
        key_pos = key_first + jnp.arange(key_block, dtype=jnp.int32)
        key_seg = lax.dynamic_slice_in_dim(seg_all, key_first, key_block, 0)
        allowed = (key_pos[None, :] <= row_pos[:, None]) & (key_seg[None, :] == row_seg[:, None])
        return jnp.where(allowed[None], scores, -jnp.inf)

    def max_step(index, running):
        return jnp.maximum(running, jnp.max(block_scores(index), axis=-1))

    row_max = lax.fori_loop(0, block_count, max_step, sink_rows)

    def sum_step(index, carried):
        weighted, denom = carried
        probs = jnp.exp(block_scores(index) - row_max[..., None]).astype(jnp.bfloat16)
        value_part = lax.dynamic_slice_in_dim(value_by_head, index * key_block, key_block, 1)
        weighted = weighted + jnp.einsum(
            "hrk,hkd->hrd", probs, value_part, preferred_element_type=jnp.float32
        )
        denom = denom + jnp.sum(probs, axis=-1, dtype=jnp.float32)
        return (weighted, denom)

    init_pair = (
        jnp.zeros((kv_heads, row_total, HEAD_SIZE), jnp.float32),
        jnp.zeros((kv_heads, row_total), jnp.float32),
    )
    weighted, denom = lax.fori_loop(0, block_count, sum_step, init_pair)
    denom = denom + jnp.exp(sink_rows - row_max)
    mixed = (weighted / denom[..., None]).astype(jnp.bfloat16)
    mixed = (
        mixed.reshape(kv_heads, heads_per_group, tok_count, HEAD_SIZE)
        .transpose(2, 0, 1, 3)
        .reshape(tok_count, query_cols)
    )
    out_terms_t = jnp.einsum(
        "efc,tc->eft", out_weight_t, mixed, preferred_element_type=jnp.float32
    )[:, :shard_rows]
    model_width = out_terms_t.shape[0] * out_terms_t.shape[1]
    out_pieces = out_terms_t.astype(jnp.bfloat16).reshape(mp_devs, model_width // mp_devs, tok_count)
    out_got = lax.all_to_all(out_pieces, "mp", split_axis=0, concat_axis=0, tiled=True)
    attn_part = jnp.sum(out_got.astype(jnp.float32), axis=0).T
    first_out = (local_rows.astype(jnp.float32) + attn_part).astype(jnp.bfloat16)
    top_count = routes.shape[2]
    local_experts = expert_in.shape[0]
    expert_count = local_experts * expert_devs
    capacity = 3 * tok_count * top_count // (2 * expert_count)
    chosen = routes[0].reshape(tok_count * top_count)
    onehot = (chosen[:, None] == jnp.arange(expert_count, dtype=jnp.int32)[None, :]).astype(
        jnp.int32
    )
    ranks = jnp.sum((jnp.cumsum(onehot, axis=0) - onehot) * onehot, axis=1)
    target = chosen * capacity + ranks
    source_row = (
        jnp.full((expert_count * capacity,), tok_count, jnp.int32)
        .at[target]
        .set(jnp.arange(tok_count * top_count, dtype=jnp.int32) // top_count)
    )
    padded = jnp.concatenate(
        [first_out, jnp.zeros((1, first_out.shape[1]), jnp.bfloat16)], axis=0
    )
    pick = (source_row[:, None] == jnp.arange(tok_count + 1, dtype=jnp.int32)[None, :]).astype(
        jnp.bfloat16
    )
    outgoing = (
        jnp.dot(pick, padded, preferred_element_type=jnp.float32)
        .astype(jnp.bfloat16)
        .reshape(expert_count, capacity, padded.shape[1])
    )
    arrived = lax.all_to_all(outgoing, "expert", split_axis=0, concat_axis=0, tiled=True)
    arrived_rows = arrived.reshape(expert_count * capacity, arrived.shape[2])
    inputs = rms_norm(lax.all_gather(arrived_rows, "mp", axis=1, tiled=True), moe_gain)
    w_in = expert_in[0]
    hidden_cols = w_in.shape[2]
    inputs = lax.optimization_barrier(inputs)
    gate_up = jnp.dot(
        inputs, jnp.concatenate([w_in[0], w_in[1]], axis=1), preferred_element_type=jnp.float32
    )
    gate_val = gate_up[:, :hidden_cols]
    up_val = gate_up[:, hidden_cols:]
    gate_val = jnp.minimum(gate_val, clamp_limit)
    up_val = jnp.clip(up_val, -clamp_limit, clamp_limit)
    activated = ((up_val + 1.0) * gate_val * jax.nn.sigmoid(glu_alpha * gate_val)).astype(
        jnp.bfloat16
    )
    activated = lax.optimization_barrier(activated)
    partials = jnp.einsum(
        "rh,hjf->jrf",
        activated,
        expert_down[0].reshape(expert_down.shape[1], mp_devs, -1),
        preferred_element_type=jnp.float32,
    )
    expert_out = lax.psum_scatter(
        partials.astype(jnp.bfloat16).reshape(mp_devs, expert_count, capacity, -1),
        "mp",
        scatter_dimension=0,
    )
    local_width = expert_out.shape[2]
    returned = lax.all_to_all(expert_out, "expert", split_axis=0, concat_axis=0, tiled=True)
    slot_pick = (
        target[:, None] == jnp.arange(expert_count * capacity, dtype=jnp.int32)[None, :]
    ).astype(jnp.bfloat16)
    picked = jnp.dot(
        slot_pick,
        returned.reshape(expert_count * capacity, local_width),
        preferred_element_type=jnp.float32,
    ).reshape(tok_count, top_count, local_width)
    moe_sum = jnp.sum(picked.astype(jnp.float32) * route_weights[0][..., None], axis=1)
    hidden = (first_out.astype(jnp.float32) + moe_sum).astype(jnp.bfloat16)
    return (hidden[None], key_rotary[None], value_fresh[None])


def solution(mesh):
    placed = (
        P("batch", "expert", "mp"),
        P("batch", None),
        P(),
        P("expert", "mp"),
        P("expert", "mp"),
        P("expert", "mp"),
        P("mp", "expert"),
        P("mp"),
        P(),
        P("expert", None, None, "mp"),
        P("expert", "mp", None),
        P("batch", "expert", None),
        P("batch", "expert", None),
    )
    return jax.shard_map(
        shards,
        mesh=mesh,
        in_specs=placed,
        out_specs=(
            P("batch", "expert", "mp"),
            P("batch", "expert", "mp"),
            P("batch", "expert", "mp"),
        ),
        check_vma=False,
    )
```
